512 devices in a mesh: cache: 32 (over x_hi, z, core), dp: 16 (over y, x_lo).
Axes of the slice: x: 4 (x_hi: 2, x_lo: 2; x = x_hi * 2 + x_lo), y: 8, z: 8, core: 2. Of those that a mesh axis runs over, the one named last changes fastest.
Arguments:
- tokens: bfloat16 [4096, 2048], P('dp', 'cache'), may hold values from -6 to 6
- gate_values: bfloat16 [4096, 2048], P('dp', 'cache'), may hold values from -6 to 6
- output_grad: bfloat16 [4096, 2048], P('dp', 'cache'), may hold values from -12 to 12
- query_weight: bfloat16 [2048, 2048], P(None, 'cache'), may hold values from -6 to 6
- master: float32 [2048, 2048], P('dp', 'cache'), may hold values from -6 to 6
- moment: float32 [2048, 2048], P('dp', 'cache'), may hold values from -6 to 6
- second: float32 [2048, 2048], P('dp', 'cache'), may hold values from 0.5 to 2
- key_codes: bfloat16 [32, 8192, 2048], P('dp', 'cache'), may hold values from -30 to 30
- value_codes: bfloat16 [32, 8192, 2048], P('dp', 'cache'), may hold values from -6 to 6
- key_scales: float32 [32, 256, 16], P('dp', 'cache'), may hold values from 0.25 to 2
- value_scales: float32 [32, 256, 16], P('dp', 'cache'), may hold values from 0.25 to 2
- span_keys: bfloat16 [4096, 2048], P(('dp', 'cache')), may hold values from -6 to 6
- span_values: bfloat16 [4096, 2048], P(('dp', 'cache')), may hold values from -6 to 6
- lengths: int32 [32], P('dp'), may hold values from 1 to 8192, 131072 in all
- segments: int32 [16, 256], P('dp'), may hold values from 0 to 1, never falling along the last dimension, each value on 1 to 192 neighbouring positions
Outputs:
- layer_output: bfloat16 [4096, 2048], P('dp', 'cache')
- new_weight: bfloat16 [2048, 2048], P(None, 'cache')
- new_master: float32 [2048, 2048], P('dp', 'cache')
- new_moment: float32 [2048, 2048], P('dp', 'cache')
- new_second: float32 [2048, 2048], P('dp', 'cache')
The draws below stay inside these ranges and needn't reach their ends.
Inputs may be any that keep to these rules, and one draw needn't show every extreme that they name: `segments`: in every row the ids never fall, every one of the 2 ids appears, each on at most three quarters of the 256 events. The lengths sum to 32 * 4096 and the largest is exactly 8192.
All inputs are finite; a program needn't handle non-finite values. No bound on the sum of `lengths` on one device may be relied on, other than what follows from the above.
Results may differ from the reference program's by a relative error of at most 0.0058.
The reference program's roundings to bfloat16 on the way (of `queries`, `attn`, `mixed_grad`, `score_grad` and `pre_grad`) count: a program that leaves them out, or rounds other values in their place, can miss the bound.
Values may be sent and summed in bfloat16 or wider, within the bound.
No kernel may reach another device: no remote copies, remote signals or barrier semaphores. Data moves between devices by JAX's collectives and lax.ppermute only.
A program may use at most 128 MiB of HBM per device.

```python
import math
import jax
import jax.numpy as jnp
import numpy as np
from jax import lax

D = 2048
HEADS = 16
TOK_GRP = 256
USERS = 2
HIST_DEV = 256
BLK = 32
STEP = 20
GROUPS = 16
TOKENS = 4096
USERS_ALL = 32
HIST = 8192
SPAN_DEV = 8
SCALE_ROWS = 256
N_CACHE = 32


def draw_key_codes(key, part):
    column = jnp.arange(D, dtype=jnp.float32) / (D - 1)
    noise = jnp.clip(jax.random.normal(key, (USERS_ALL, HIST, D), jnp.float32), -6.0, 6.0)
    tilt = 1.0 + 2.0 * column
    return (noise * tilt[None, None, :]).astype(jnp.bfloat16)


def level_of(own_key, shape, cuts, smallest, high):
    factor_of, own = 1.0, jax.random.fold_in(own_key, 6)
    for dim, blocks in cuts:
        draws = jnp.exp(jax.random.uniform(jax.random.fold_in(own, dim), (blocks,), jnp.float32, smallest / len(cuts), high / len(cuts)))
        factor_of = factor_of * jnp.repeat(draws, shape[dim] // blocks).reshape([-1 if axis == dim else 1 for axis in range(len(shape))])
    return factor_of


def split_up(amount, total, bound, skew):
    loads = [(1 << 20) // math.isqrt(standing ** skew) + 1 for standing in range(2, amount + 1)]
    surplus, given = total - bound - (amount - 1), [1] * (amount - 1)
    while surplus > 0:
        candidates = [i for i in range(amount - 1) if given[i] < bound]
        whole, budget = sum([loads[i] for i in candidates]), surplus
        for i in candidates:
            more = min(bound - given[i], max(1, budget * loads[i] // whole), surplus)
            given[i] = given[i] + more
            surplus = surplus - more
    return np.array([bound] + given)


def ragged(stream_key, number_of, total, limit, lean):
    if number_of == 2:
        one = jax.random.randint(stream_key, (), max(1, total - limit), min(limit, total - 1) + 1)
        return jnp.stack([one, total - one])
    sizes = jnp.asarray(split_up(number_of, total, limit, lean), jnp.int32)
    pairs = (number_of - 1) // 2
    source_of, sink = sizes[1:1 + 2 * pairs:2], sizes[2:2 + 2 * pairs:2]
    margin = jnp.minimum(source_of - 1, limit - sink)
    moved = jax.random.randint(jax.random.fold_in(stream_key, 1), (pairs,), 0, 1 << 20) % (margin + 1)
    sizes = sizes.at[1:1 + 2 * pairs:2].set(source_of - moved).at[2:2 + 2 * pairs:2].set(sink + moved)
    return sizes[jax.random.permutation(jax.random.fold_in(stream_key, 2), number_of)]


def gaussian(own_key, dims, spread, limit, cuts=(), kind=jnp.bfloat16):
    array = spread * jax.random.normal(own_key, dims, jnp.float32)
    if cuts:
        array = array * level_of(own_key, dims, cuts, -0.22, 0.18)
    return jnp.clip(array, -limit, limit).astype(kind)


def setup_inputs(seed: int = 0) -> dict:
    arg_keys = jax.random.split(jax.random.key(seed), 16)
    tokens = gaussian(arg_keys[0], (TOKENS, D), 1.0, 6.0, ((0, 16), (1, 32)))
    gate_values = gaussian(arg_keys[1], (TOKENS, D), 1.0, 6.0, ((0, 16), (1, 32)))
    output_grad = gaussian(arg_keys[2], (TOKENS, D), 2.0, 12.0, ((0, 16), (1, 32)))
    query_weight = gaussian(arg_keys[3], (D, D), 1.0, 6.0, ((1, 32),))
    master = gaussian(arg_keys[4], (D, D), 1.0, 6.0, ((0, 16), (1, 32)), jnp.float32)
    moment = gaussian(arg_keys[5], (D, D), 1.0, 6.0, ((0, 16), (1, 32)), jnp.float32)
    second = jnp.clip(jnp.exp(math.log(2.0) - 1.3862944 * jax.random.uniform(arg_keys[6], (D, D), jnp.float32) ** level_of(arg_keys[6], (D, D), ((0, 16), (1, 32)), -0.2, 0.2)), 0.5, 2.0)
    key_codes = draw_key_codes(jax.random.fold_in(arg_keys[15], 71), 0)
    value_codes = gaussian(arg_keys[8], (USERS_ALL, HIST, D), 1.0, 6.0, ((0, 16), (1, 32)))
    key_scales = jnp.clip(jnp.exp(math.log(2.0) - 2.0794415 * jax.random.uniform(arg_keys[9], (USERS_ALL, SCALE_ROWS, HEADS), jnp.float32) ** level_of(arg_keys[9], (USERS_ALL, SCALE_ROWS, HEADS), ((0, 16), (1, 32)), -0.2, 0.2)), 0.25, 2.0)
    value_scales = jnp.clip(jnp.exp(math.log(2.0) - 2.0794415 * jax.random.uniform(arg_keys[10], (USERS_ALL, SCALE_ROWS, HEADS), jnp.float32) ** level_of(arg_keys[10], (USERS_ALL, SCALE_ROWS, HEADS), ((0, 16), (1, 32)), -0.2, 0.2)), 0.25, 2.0)
    span_keys = gaussian(arg_keys[11], (TOKENS, D), 1.0, 6.0, ((0, 512),))
    span_values = gaussian(arg_keys[12], (TOKENS, D), 1.0, 6.0, ((0, 512),))
    lengths = ragged(arg_keys[13], USERS_ALL, USERS_ALL * HIST // 2, HIST, 0).astype(jnp.int32)
    segments = jax.vmap(lambda own: jnp.searchsorted(jnp.cumsum(ragged(own, USERS, TOK_GRP, TOK_GRP * 3 // 4, 0)), jnp.arange(TOK_GRP), side="right"))(jax.random.split(arg_keys[14], GROUPS)).reshape((GROUPS, TOK_GRP)).astype(jnp.int32)
    return dict(tokens=tokens, gate_values=gate_values, output_grad=output_grad, query_weight=query_weight, master=master, moment=moment, second=second, key_codes=key_codes, value_codes=value_codes, key_scales=key_scales, value_scales=value_scales, span_keys=span_keys, span_values=span_values, lengths=lengths, segments=segments)


def silu_slope(values):
    sigmoid_value = jax.nn.sigmoid(values)
    return sigmoid_value * (1.0 + values * (1.0 - sigmoid_value))

def product(form, left, right):
    return jnp.einsum(form, left.astype(jnp.float32), right.astype(jnp.float32), precision=lax.Precision.HIGHEST)

def dequantize(stored, scales):
    user_count, row_count, model_width = stored.shape
    block_count, head_count = (scales.shape[1], scales.shape[2])
    shaped = stored.astype(jnp.float32).reshape(user_count, block_count, row_count // block_count, head_count, model_width // head_count)
    scaled = shaped * scales[:, :, None, :, None]
    return scaled.astype(jnp.bfloat16).reshape(user_count * row_count, model_width)

def key_mask(user_ids, lengths, shard_index, hist_rows, span_rows):
    query_count = user_ids.shape[0]
    user_count = lengths.shape[0]
    key_index = jnp.arange(user_count * hist_rows, dtype=jnp.int32)
    key_user = key_index // hist_rows
    key_row = shard_index * hist_rows + key_index % hist_rows
    user_range = jnp.arange(user_count, dtype=jnp.int32)
    key_limit = lax.optimization_barrier(jnp.sum(jnp.where(key_user[:, None] == user_range[None, :], lengths[None, :], 0), axis=1))
    history_mask = (user_ids[:, None] == key_user[None, :]) & (key_row < key_limit)[None, :]
    span_start = (shard_index * span_rows).astype(jnp.int32)
    span_pos = span_start + jnp.arange(span_rows, dtype=jnp.int32)
    span_users = lax.dynamic_slice_in_dim(user_ids, span_start, span_rows, 0)
    query_pos = jnp.arange(query_count, dtype=jnp.int32)
    span_mask = (user_ids[:, None] == span_users[None, :]) & (span_pos[None, :] <= query_pos[:, None])
    return jnp.concatenate([history_mask, span_mask], axis=1)

def split_heads(matrix, head_count):
    return matrix.reshape(matrix.shape[0], head_count, matrix.shape[1] // head_count)

def forward_part(queries, keys, values_all, mask, head_count):
    head_size = queries.shape[1] // head_count
    scores = product('qhd,khd->hqk', split_heads(queries, head_count), split_heads(keys, head_count)) / math.sqrt(head_size)
    attn = jnp.where(mask[None], jax.nn.silu(scores), 0.0).astype(jnp.bfloat16)
    mixed = product('hqk,khd->qhd', attn, split_heads(values_all, head_count))
    return mixed.reshape(queries.shape[0], queries.shape[1])

def backward_part(queries, keys, values_all, mask, mixed_grad, head_count):
    head_size = queries.shape[1] // head_count
    scores = product('qhd,khd->hqk', split_heads(queries, head_count), split_heads(keys, head_count)) / math.sqrt(head_size)
    attn_grad = product('qhd,khd->hqk', split_heads(mixed_grad, head_count), split_heads(values_all, head_count))
    score_grad = jnp.where(mask[None], attn_grad * silu_slope(scores), 0.0) / math.sqrt(head_size)
    score_grad = score_grad.astype(jnp.bfloat16)
    query_grad = product('hqk,khd->qhd', score_grad, split_heads(keys, head_count))
    return query_grad.reshape(queries.shape[0], queries.shape[1])

def group_terms(packed):
    group_queries, user_ids, group_lengths, key_codes, value_codes, key_scales, value_scales, span_keys, span_values, gate_group, grad_group = packed
    blocks_dev = HIST_DEV // BLK

    def shard_keys(shard_index):
        start = (shard_index * HIST_DEV).astype(jnp.int32)
        block_start = (shard_index * blocks_dev).astype(jnp.int32)
        span_start = (shard_index * SPAN_DEV).astype(jnp.int32)
        keys = jnp.concatenate([dequantize(lax.dynamic_slice_in_dim(key_codes, start, HIST_DEV, 1), lax.dynamic_slice_in_dim(key_scales, block_start, blocks_dev, 1)), lax.dynamic_slice_in_dim(span_keys, span_start, SPAN_DEV, 0)], axis=0)
        values_all = jnp.concatenate([dequantize(lax.dynamic_slice_in_dim(value_codes, start, HIST_DEV, 1), lax.dynamic_slice_in_dim(value_scales, block_start, blocks_dev, 1)), lax.dynamic_slice_in_dim(span_values, span_start, SPAN_DEV, 0)], axis=0)
        mask = key_mask(user_ids, group_lengths, shard_index, HIST_DEV, SPAN_DEV)
        return (keys, values_all, mask)

    def forward_step(total, shard_index):
        keys, values_all, mask = shard_keys(shard_index)
        return (total + forward_part(group_queries, keys, values_all, mask, HEADS), None)
    empty = jnp.zeros((TOK_GRP, D), jnp.float32)
    shard_list = jnp.arange(N_CACHE, dtype=jnp.int32)
    mixed, _ = lax.scan(forward_step, empty, shard_list)
    row_mean = lax.optimization_barrier(jnp.mean(mixed, axis=1, keepdims=True))
    centered = mixed - row_mean
    row_var = lax.optimization_barrier(jnp.mean(centered * centered, axis=1, keepdims=True))
    inverse = 1.0 / jnp.sqrt(row_var + 1e-05)
    normed = centered * inverse
    gate_float = gate_group.astype(jnp.float32)
    layer_output = (gate_float * normed).astype(jnp.bfloat16)
    back = grad_group.astype(jnp.float32) * gate_float
    mixed_grad = inverse * (back - lax.optimization_barrier(jnp.mean(back, axis=1, keepdims=True)) - normed * lax.optimization_barrier(jnp.mean(back * normed, axis=1, keepdims=True)))
    mixed_grad = mixed_grad.astype(jnp.bfloat16)

    def backward_step(total, shard_index):
        keys, values_all, mask = shard_keys(shard_index)
        part = backward_part(group_queries, keys, values_all, mask, mixed_grad, HEADS)
        rounded = lax.optimization_barrier(part.astype(jnp.bfloat16))
        return (total + rounded.astype(jnp.float32), None)
    query_grad, _ = lax.scan(backward_step, empty, shard_list)
    return (layer_output, query_grad)

def reference(tokens, gate_values, output_grad, query_weight, master, moment, second, key_codes, value_codes, key_scales, value_scales, span_keys, span_values, lengths, segments):
    query_pre = jnp.dot(tokens, query_weight, preferred_element_type=jnp.float32) / math.sqrt(D)
    queries = jax.nn.silu(query_pre).astype(jnp.bfloat16)
    packed = (queries.reshape(GROUPS, TOK_GRP, D), segments, lengths.reshape(GROUPS, USERS), key_codes.reshape(GROUPS, USERS, HIST, D), value_codes.reshape(GROUPS, USERS, HIST, D), key_scales.reshape(GROUPS, USERS, SCALE_ROWS, HEADS), value_scales.reshape(GROUPS, USERS, SCALE_ROWS, HEADS), span_keys.reshape(GROUPS, TOK_GRP, D), span_values.reshape(GROUPS, TOK_GRP, D), gate_values.reshape(GROUPS, TOK_GRP, D), output_grad.reshape(GROUPS, TOK_GRP, D))
    outputs, query_grad = lax.map(group_terms, packed)
    layer_output = outputs.reshape(TOKENS, D)
    pre_grad = (query_grad.reshape(TOKENS, D) * silu_slope(query_pre)).astype(jnp.bfloat16)
    weight_grad = lax.dot_general(tokens, pre_grad, (((0,), (0,)), ((), ())), preferred_element_type=jnp.float32) / math.sqrt(D)
    square_total = jnp.sum(weight_grad * weight_grad)
    grad_level = jnp.sqrt(square_total / (D * D))
    clip_factor = jnp.minimum(1.0, 0.5 / (grad_level + 1e-06))
    clipped = clip_factor * weight_grad
    new_moment = 0.9 * moment + 0.1 * clipped
    new_second = 0.95 * second + 0.05 * clipped * clipped
    first_fix = new_moment / (1.0 - 0.9 ** STEP)
    second_fix = new_second / (1.0 - 0.95 ** STEP)
    new_master = master - 0.01 * (first_fix / (jnp.sqrt(second_fix) + 1e-08) + 0.1 * master)
    new_weight = new_master.astype(jnp.bfloat16)
    return (layer_output, new_weight, new_master, new_moment, new_second)
```

```python
import math

import jax
import jax.numpy as jnp
from jax import lax
from jax.sharding import Mesh
from jax.sharding import PartitionSpec as P

HEADS = 16
STEP = 20
CACHE = ("cache_0", "cache_1", "cache_2")
DP = ("dp_0", "dp_1")
CACHE_DP = ("cache_0", "cache_1", "cache_2", "dp_0", "dp_1")
DP_CACHE = ("dp_0", "dp_1", "cache_0", "cache_1", "cache_2")


def split_up(array, dim, peers):
    dims = array.shape
    tiles = array.reshape(*dims[:dim], peers, dims[dim] // peers, *dims[dim + 1 :])
    return jnp.moveaxis(tiles, dim, 0)


def summed_on_arrival(array, axis, dim):
    tiles = split_up(array, dim, lax.axis_size(axis))
    arrived = lax.all_to_all(tiles, axis, split_axis=0, concat_axis=0, tiled=True)
    return arrived.sum(axis=0)


def sent_to_all(array, axis):
    copies = jnp.broadcast_to(array, (lax.axis_size(axis), *array.shape))
    return lax.all_to_all(copies, axis, split_axis=0, concat_axis=0, tiled=True)


def of_everyone(array, axis):
    everything = sent_to_all(array, axis)
    return jnp.sum(everything, axis=0)


def packed_total(arrays, axis):
    flat, at, outs = (jnp.concatenate([a.reshape(-1) for a in arrays]), 0, [])
    subtotal = of_everyone(flat, axis)
    for a in arrays:
        outs.append(subtotal[at : at + a.size].reshape(a.shape))
        at += a.size
    return tuple(outs)


def in_order(tiles, dim):
    dims = list(tiles.shape[1:])
    dims[dim] *= tiles.shape[0]
    return jnp.moveaxis(tiles, 0, dim).reshape(dims)


def collect(array, axis, dim):
    tiles = sent_to_all(array, axis)
    return in_order(tiles, dim)


def sent_and_summed(array, axis, dim):
    peers = lax.axis_size(axis)
    tiles = lax.all_to_all(split_up(array, dim, peers), axis, 0, 0, tiled=True)
    return jnp.sum(tiles.astype(jnp.float32), axis=0)


def by_axis(array, axes):
    for axis in axes:
        array = lax.psum(array, axis)
    return array


def silu_slope(values):
    sigmoid_value = jax.nn.sigmoid(values)
    return sigmoid_value * (1.0 + values * (1.0 - sigmoid_value))


def product(form, left, right):
    return jnp.einsum(form, left, right, preferred_element_type=jnp.float32)


def dequantize(stored, scales):
    user_count, row_count, model_width = stored.shape
    block_count, head_count = (scales.shape[1], scales.shape[2])
    shaped = stored.astype(jnp.float32).reshape(
        user_count, block_count, row_count // block_count, head_count, model_width // head_count
    )
    scaled = shaped * scales[:, :, None, :, None]
    return scaled.astype(jnp.bfloat16).reshape(user_count * row_count, model_width)


def key_mask(user_ids, lengths, shard_index, hist_rows, span_rows):
    query_count = user_ids.shape[0]
    user_count = lengths.shape[0]
    key_index = jnp.arange(user_count * hist_rows, dtype=jnp.int32)
    key_user = key_index // hist_rows
    key_row = shard_index * hist_rows + key_index % hist_rows
    user_range = jnp.arange(user_count, dtype=jnp.int32)
    key_limit = jnp.sum(
        jnp.where(key_user[:, None] == user_range[None, :], lengths[None, :], 0), axis=1
    )
    history_mask = (user_ids[:, None] == key_user[None, :]) & (key_row < key_limit)[None, :]
    span_start = shard_index * span_rows
    span_pos = span_start + jnp.arange(span_rows, dtype=jnp.int32)
    span_users = lax.dynamic_slice_in_dim(user_ids, span_start, span_rows, 0)
    query_pos = jnp.arange(query_count, dtype=jnp.int32)
    span_mask = (user_ids[:, None] == span_users[None, :]) & (
        span_pos[None, :] <= query_pos[:, None]
    )
    return jnp.concatenate([history_mask, span_mask], axis=1)


def split_heads(matrix, head_count):
    return matrix.reshape(matrix.shape[0], head_count, matrix.shape[1] // head_count)


def forward_part(queries, keys, values_all, mask, head_count):
    head_size = queries.shape[1] // head_count
    scores = product(
        "qhd,khd->hqk", split_heads(queries, head_count), split_heads(keys, head_count)
    ) / math.sqrt(head_size)
    attn = jnp.where(mask[None], jax.nn.silu(scores), 0.0).astype(jnp.bfloat16)
    mixed = product("hqk,khd->qhd", attn, split_heads(values_all, head_count))
    weighted_slope = jnp.where(mask[None], silu_slope(scores), 0.0) / math.sqrt(head_size)
    return (mixed.reshape(queries.shape[0], queries.shape[1]), weighted_slope)


def backward_part(keys, values_all, weighted_slope, mixed_grad, head_count):
    attn_grad = product(
        "qhd,khd->hqk", split_heads(mixed_grad, head_count), split_heads(values_all, head_count)
    )
    score_grad = (attn_grad * weighted_slope).astype(jnp.bfloat16)
    query_grad = product("hqk,khd->qhd", score_grad, split_heads(keys, head_count))
    return query_grad.reshape(mixed_grad.shape[0], mixed_grad.shape[1])


def shards(
    tokens,
    gate_values,
    output_grad,
    query_weight,
    master,
    moment,
    second,
    key_codes,
    value_codes,
    key_scales,
    value_scales,
    span_keys,
    span_values,
    lengths,
    segments,
):
    model_width = query_weight.shape[0]
    shard_index = lax.axis_index(CACHE)
    features = collect(tokens, CACHE, 1)
    query_pre = jnp.dot(features, query_weight, preferred_element_type=jnp.float32) / math.sqrt(
        model_width
    )
    query_block = jax.nn.silu(query_pre).astype(jnp.bfloat16)
    queries = collect(query_block, CACHE, 1)
    user_ids = segments[0]
    hist_rows = key_codes.shape[1]
    span_rows = span_keys.shape[0]
    keys = jnp.concatenate([dequantize(key_codes, key_scales), span_keys], axis=0)
    values_all = jnp.concatenate([dequantize(value_codes, value_scales), span_values], axis=0)
    mask = key_mask(user_ids, lengths, shard_index, hist_rows, span_rows)
    mixed_part, weighted_slope = forward_part(queries, keys, values_all, mask, HEADS)
    gate_float = gate_values.astype(jnp.float32)
    mixed_block = summed_on_arrival(mixed_part, CACHE, 1)
    back = output_grad.astype(jnp.float32) * gate_float
    row_sum, row_square, back_sum, back_mixed = packed_total(
        (
            jnp.sum(mixed_block, axis=1),
            jnp.sum(mixed_block * mixed_block, axis=1),
            jnp.sum(back, axis=1),
            jnp.sum(back * mixed_block, axis=1),
        ),
        CACHE,
    )
    row_mean = (row_sum / model_width)[:, None]
    row_var = (row_square / model_width)[:, None] - row_mean * row_mean
    inverse = 1.0 / jnp.sqrt(row_var + 1e-05)
    normed = (mixed_block - row_mean) * inverse
    layer_block = (gate_float * normed).astype(jnp.bfloat16)
    back_cross = inverse[:, 0] * (back_mixed - row_mean[:, 0] * back_sum)
    grad_block = inverse * (
        back - (back_sum / model_width)[:, None] - normed * (back_cross / model_width)[:, None]
    )
    mixed_grad = collect(grad_block.astype(jnp.bfloat16), CACHE, 1)
    query_part = backward_part(keys, values_all, weighted_slope, mixed_grad, HEADS)
    query_grad = sent_and_summed(query_part.astype(jnp.bfloat16), CACHE, 1)
    pre_grad = (query_grad * silu_slope(query_pre)).astype(jnp.bfloat16)
    weight_part = lax.dot_general(
        features, pre_grad, (((0,), (0,)), ((), ())), preferred_element_type=jnp.float32
    ) / math.sqrt(model_width)
    grad_owned = sent_and_summed(weight_part.astype(jnp.bfloat16), DP, 0)
    square_total = of_everyone(jnp.sum(grad_owned * grad_owned).reshape(1), CACHE_DP)[0]
    grad_level = jnp.sqrt(square_total / (model_width * model_width))
    clip_factor = jnp.minimum(1.0, 0.5 / (grad_level + 1e-06))
    clipped = clip_factor * grad_owned
    new_moment = 0.9 * moment + 0.1 * clipped
    new_second = 0.95 * second + 0.05 * clipped * clipped
    first_fix = new_moment / (1.0 - 0.9**STEP)
    second_fix = new_second / (1.0 - 0.95**STEP)
    new_master = master - 0.01 * (first_fix / (jnp.sqrt(second_fix) + 1e-08) + 0.1 * master)
    new_weight = collect(new_master.astype(jnp.bfloat16), DP, 0)
    return (layer_block, new_weight, new_master, new_moment, new_second)


def solution(mesh):
    torus = Mesh(
        mesh.devices.reshape(2, 8, 2, 8, 2), ("cache_0", "cache_1", "cache_2", "dp_0", "dp_1")
    )
    placed = (
        P(DP, CACHE),
        P(DP, CACHE),
        P(DP, CACHE),
        P(None, CACHE),
        P(DP, CACHE),
        P(DP, CACHE),
        P(DP, CACHE),
        P(DP, CACHE, None),
        P(DP, CACHE, None),
        P(DP, CACHE, None),
        P(DP, CACHE, None),
        P(DP_CACHE, None),
        P(DP_CACHE, None),
        P(DP),
        P(DP, None),
    )
    return jax.shard_map(
        shards,
        mesh=torus,
        in_specs=placed,
        out_specs=(P(DP, CACHE), P(None, CACHE), P(DP, CACHE), P(DP, CACHE), P(DP, CACHE)),
        check_vma=False,
    )
```

```python
import math

import jax
import jax.numpy as jnp
from jax import lax
from jax.sharding import Mesh
from jax.sharding import PartitionSpec as P

HEADS = 16
STEP = 20
CACHE = ("cache_0", "cache_1", "cache_2")
DP = ("dp_0", "dp_1")
CACHE_DP = ("cache_0", "cache_1", "cache_2", "dp_0", "dp_1")
DP_CACHE = ("dp_0", "dp_1", "cache_0", "cache_1", "cache_2")


def split_up(array, dim, peers):
    dims = array.shape
    tiles = array.reshape(*dims[:dim], peers, dims[dim] // peers, *dims[dim + 1 :])
    return jnp.moveaxis(tiles, dim, 0)


def summed_on_arrival(array, axis, dim):
    tiles = split_up(array, dim, lax.axis_size(axis))
    arrived = lax.all_to_all(tiles, axis, split_axis=0, concat_axis=0, tiled=True)
    return arrived.sum(axis=0)


def sent_to_all(array, axis):
    copies = jnp.broadcast_to(array, (lax.axis_size(axis), *array.shape))
    return lax.all_to_all(copies, axis, split_axis=0, concat_axis=0, tiled=True)


def of_everyone(array, axis):
    everything = sent_to_all(array, axis)
    return jnp.sum(everything, axis=0)


def packed_total(arrays, axis):
    flat, at, outs = (jnp.concatenate([a.reshape(-1) for a in arrays]), 0, [])
    subtotal = of_everyone(flat, axis)
    for a in arrays:
        outs.append(subtotal[at : at + a.size].reshape(a.shape))
        at += a.size
    return tuple(outs)


def in_order(tiles, dim):
    dims = list(tiles.shape[1:])
    dims[dim] *= tiles.shape[0]
    return jnp.moveaxis(tiles, 0, dim).reshape(dims)


CHIPS = ("cache_0", "cache_1")
CORE = "cache_2"


def collect_cache(array, dim):
    chips = lax.axis_size(CHIPS)
    across = lax.all_to_all(
        jnp.broadcast_to(array, (chips, *array.shape)), CHIPS, 0, 0, tiled=True
    )
    cores = lax.axis_size(CORE)
    pairs = lax.all_to_all(
        jnp.broadcast_to(across, (cores, *across.shape)), CORE, 0, 0, tiled=True
    )
    tiles = jnp.swapaxes(pairs, 0, 1).reshape(chips * cores, *array.shape)
    return in_order(tiles, dim)


def summed_over_cache(array, dim):
    chips, cores = (lax.axis_size(CHIPS), lax.axis_size(CORE))
    tiles = split_up(array, dim, chips * cores)
    tiles = jnp.swapaxes(tiles.reshape(chips, cores, *tiles.shape[1:]), 0, 1)
    on_chip = lax.all_to_all(tiles, CORE, 0, 0, tiled=True).sum(axis=0)
    return lax.all_to_all(on_chip, CHIPS, 0, 0, tiled=True).sum(axis=0)


def collect(array, axis, dim):
    tiles = sent_to_all(array, axis)
    return in_order(tiles, dim)


def sent_and_summed(array, axis, dim):
    peers = lax.axis_size(axis)
    tiles = lax.all_to_all(split_up(array, dim, peers), axis, 0, 0, tiled=True)
    return jnp.sum(tiles.astype(jnp.float32), axis=0)


def by_axis(array, axes):
    for axis in axes:
        array = lax.psum(array, axis)
    return array


def silu_slope(values):
    sigmoid_value = jax.nn.sigmoid(values)
    return sigmoid_value * (1.0 + values * (1.0 - sigmoid_value))


def product(form, left, right):
    return jnp.einsum(form, left, right, preferred_element_type=jnp.float32)


def dequantize(stored, scales):
    user_count, row_count, model_width = stored.shape
    block_count, head_count = (scales.shape[1], scales.shape[2])
    shaped = stored.astype(jnp.float32).reshape(
        user_count, block_count, row_count // block_count, head_count, model_width // head_count
    )
    scaled = shaped * scales[:, :, None, :, None]
    return scaled.astype(jnp.bfloat16).reshape(user_count * row_count, model_width)


def key_mask(user_ids, lengths, shard_index, hist_rows, span_rows):
    query_count = user_ids.shape[0]
    user_count = lengths.shape[0]
    key_index = jnp.arange(user_count * hist_rows, dtype=jnp.int32)
    key_user = key_index // hist_rows
    key_row = shard_index * hist_rows + key_index % hist_rows
    user_range = jnp.arange(user_count, dtype=jnp.int32)
    key_limit = jnp.sum(
        jnp.where(key_user[:, None] == user_range[None, :], lengths[None, :], 0), axis=1
    )
    history_mask = (user_ids[:, None] == key_user[None, :]) & (key_row < key_limit)[None, :]
    span_start = shard_index * span_rows
    span_pos = span_start + jnp.arange(span_rows, dtype=jnp.int32)
    span_users = lax.dynamic_slice_in_dim(user_ids, span_start, span_rows, 0)
    query_pos = jnp.arange(query_count, dtype=jnp.int32)
    span_mask = (user_ids[:, None] == span_users[None, :]) & (
        span_pos[None, :] <= query_pos[:, None]
    )
    return jnp.concatenate([history_mask, span_mask], axis=1)


def split_heads(matrix, head_count):
    return matrix.reshape(matrix.shape[0], head_count, matrix.shape[1] // head_count)


def forward_part(queries, keys, values_all, mask, head_count):
    head_size = queries.shape[1] // head_count
    scores = product(
        "qhd,khd->hqk", split_heads(queries, head_count), split_heads(keys, head_count)
    ) / math.sqrt(head_size)
    attn = jnp.where(mask[None], jax.nn.silu(scores), 0.0).astype(jnp.bfloat16)
    mixed = product("hqk,khd->qhd", attn, split_heads(values_all, head_count))
    weighted_slope = jnp.where(mask[None], silu_slope(scores), 0.0) / math.sqrt(head_size)
    return (mixed.reshape(queries.shape[0], queries.shape[1]), weighted_slope)


def backward_part(keys, values_all, weighted_slope, mixed_grad, head_count):
    attn_grad = product(
        "qhd,khd->hqk", split_heads(mixed_grad, head_count), split_heads(values_all, head_count)
    )
    score_grad = (attn_grad * weighted_slope).astype(jnp.bfloat16)
    query_grad = product("hqk,khd->qhd", score_grad, split_heads(keys, head_count))
    return query_grad.reshape(mixed_grad.shape[0], mixed_grad.shape[1])


def shards(
    tokens,
    gate_values,
    output_grad,
    query_weight,
    master,
    moment,
    second,
    key_codes,
    value_codes,
    key_scales,
    value_scales,
    span_keys,
    span_values,
    lengths,
    segments,
):
    model_width = query_weight.shape[0]
    shard_index = lax.axis_index(CACHE)
    features = collect_cache(tokens, 1)
    query_pre = jnp.dot(features, query_weight, preferred_element_type=jnp.float32) / math.sqrt(
        model_width
    )
    query_block = jax.nn.silu(query_pre).astype(jnp.bfloat16)
    queries = collect_cache(query_block, 1)
    user_ids = segments[0]
    hist_rows = key_codes.shape[1]
    span_rows = span_keys.shape[0]
    keys = jnp.concatenate([dequantize(key_codes, key_scales), span_keys], axis=0)
    values_all = jnp.concatenate([dequantize(value_codes, value_scales), span_values], axis=0)
    mask = key_mask(user_ids, lengths, shard_index, hist_rows, span_rows)
    mixed_part, weighted_slope = forward_part(queries, keys, values_all, mask, HEADS)
    gate_float = gate_values.astype(jnp.float32)
    mixed_block = summed_over_cache(mixed_part, 1)
    back = output_grad.astype(jnp.float32) * gate_float
    row_sum, row_square, back_sum, back_mixed = packed_total(
        (
            jnp.sum(mixed_block, axis=1),
            jnp.sum(mixed_block * mixed_block, axis=1),
            jnp.sum(back, axis=1),
            jnp.sum(back * mixed_block, axis=1),
        ),
        CACHE,
    )
    row_mean = (row_sum / model_width)[:, None]
    row_var = (row_square / model_width)[:, None] - row_mean * row_mean
    inverse = 1.0 / jnp.sqrt(row_var + 1e-05)
    normed = (mixed_block - row_mean) * inverse
    layer_block = (gate_float * normed).astype(jnp.bfloat16)
    back_cross = inverse[:, 0] * (back_mixed - row_mean[:, 0] * back_sum)
    grad_block = inverse * (
        back - (back_sum / model_width)[:, None] - normed * (back_cross / model_width)[:, None]
    )
    mixed_grad = collect_cache(grad_block.astype(jnp.bfloat16), 1)
    query_part = backward_part(keys, values_all, weighted_slope, mixed_grad, HEADS)
    query_grad = sent_and_summed(query_part.astype(jnp.bfloat16), CACHE, 1)
    pre_grad = (query_grad * silu_slope(query_pre)).astype(jnp.bfloat16)
    weight_part = lax.dot_general(
        features, pre_grad, (((0,), (0,)), ((), ())), preferred_element_type=jnp.float32
    ) / math.sqrt(model_width)
    grad_owned = sent_and_summed(weight_part.astype(jnp.bfloat16), DP, 0)
    square_total = of_everyone(jnp.sum(grad_owned * grad_owned).reshape(1), CACHE_DP)[0]
    grad_level = jnp.sqrt(square_total / (model_width * model_width))
    clip_factor = jnp.minimum(1.0, 0.5 / (grad_level + 1e-06))
    clipped = clip_factor * grad_owned
    new_moment = 0.9 * moment + 0.1 * clipped
    new_second = 0.95 * second + 0.05 * clipped * clipped
    first_fix = new_moment / (1.0 - 0.9**STEP)
    second_fix = new_second / (1.0 - 0.95**STEP)
    new_master = master - 0.01 * (first_fix / (jnp.sqrt(second_fix) + 1e-08) + 0.1 * master)
    new_weight = collect(new_master.astype(jnp.bfloat16), DP, 0)
    return (layer_block, new_weight, new_master, new_moment, new_second)


def solution(mesh):
    torus = Mesh(
        mesh.devices.reshape(2, 8, 2, 8, 2), ("cache_0", "cache_1", "cache_2", "dp_0", "dp_1")
    )
    placed = (
        P(DP, CACHE),
        P(DP, CACHE),
        P(DP, CACHE),
        P(None, CACHE),
        P(DP, CACHE),
        P(DP, CACHE),
        P(DP, CACHE),
        P(DP, CACHE, None),
        P(DP, CACHE, None),
        P(DP, CACHE, None),
        P(DP, CACHE, None),
        P(DP_CACHE, None),
        P(DP_CACHE, None),
        P(DP),
        P(DP, None),
    )
    return jax.shard_map(
        shards,
        mesh=torus,
        in_specs=placed,
        out_specs=(P(DP, CACHE), P(None, CACHE), P(DP, CACHE), P(DP, CACHE), P(DP, CACHE)),
        check_vma=False,
    )
```

```python
import math

import jax
import jax.numpy as jnp
from jax import lax
from jax.sharding import Mesh
from jax.sharding import PartitionSpec as P

HEADS = 16
STEP = 20
CACHE = ("cache_0", "cache_1", "cache_2")
DP = ("dp_0", "dp_1")
CACHE_DP = ("cache_0", "cache_1", "cache_2", "dp_0", "dp_1")
DP_CACHE = ("dp_0", "dp_1", "cache_0", "cache_1", "cache_2")


def split_up(array, dim, peers):
    dims = array.shape
    tiles = array.reshape(*dims[:dim], peers, dims[dim] // peers, *dims[dim + 1 :])
    return jnp.moveaxis(tiles, dim, 0)


def summed_on_arrival(array, axis, dim):
    tiles = split_up(array, dim, lax.axis_size(axis))
    arrived = lax.all_to_all(tiles, axis, split_axis=0, concat_axis=0, tiled=True)
    return arrived.sum(axis=0)


def sent_to_all(array, axis):
    copies = jnp.broadcast_to(array, (lax.axis_size(axis), *array.shape))
    return lax.all_to_all(copies, axis, split_axis=0, concat_axis=0, tiled=True)


def of_everyone(array, axis):
    everything = sent_to_all(array, axis)
    return jnp.sum(everything, axis=0)


def packed_total(arrays, axis):
    flat, at, outs = (jnp.concatenate([a.reshape(-1) for a in arrays]), 0, [])
    subtotal = of_everyone(flat, axis)
    for a in arrays:
        outs.append(subtotal[at : at + a.size].reshape(a.shape))
        at += a.size
    return tuple(outs)


def in_order(tiles, dim):
    dims = list(tiles.shape[1:])
    dims[dim] *= tiles.shape[0]
    return jnp.moveaxis(tiles, 0, dim).reshape(dims)


CHIPS = ("cache_0", "cache_1")
CORE = "cache_2"


def collect_cache(array, dim):
    chips = lax.axis_size(CHIPS)
    across = lax.all_to_all(
        jnp.broadcast_to(array, (chips, *array.shape)), CHIPS, 0, 0, tiled=True
    )
    cores = lax.axis_size(CORE)
    pairs = lax.all_to_all(
        jnp.broadcast_to(across, (cores, *across.shape)), CORE, 0, 0, tiled=True
    )
    tiles = jnp.swapaxes(pairs, 0, 1).reshape(chips * cores, *array.shape)
    return in_order(tiles, dim)


def summed_over_cache(array, dim):
    chips, cores = (lax.axis_size(CHIPS), lax.axis_size(CORE))
    tiles = split_up(array, dim, chips * cores)
    tiles = jnp.swapaxes(tiles.reshape(chips, cores, *tiles.shape[1:]), 0, 1)
    on_chip = lax.all_to_all(tiles, CORE, 0, 0, tiled=True).sum(axis=0)
    return lax.all_to_all(on_chip, CHIPS, 0, 0, tiled=True).sum(axis=0)


def rounded_sum_over_cache(array, dim):
    chips, cores = (lax.axis_size(CHIPS), lax.axis_size(CORE))
    tiles = split_up(array.astype(jnp.bfloat16), dim, chips * cores)
    tiles = jnp.swapaxes(tiles.reshape(chips, cores, *tiles.shape[1:]), 0, 1)
    on_chip = lax.all_to_all(tiles, CORE, 0, 0, tiled=True)
    pair_sum = jnp.sum(on_chip.astype(jnp.float32), axis=0).astype(jnp.bfloat16)
    arrived = lax.all_to_all(pair_sum, CHIPS, 0, 0, tiled=True)
    return jnp.sum(arrived.astype(jnp.float32), axis=0)


def collect(array, axis, dim):
    tiles = sent_to_all(array, axis)
    return in_order(tiles, dim)


def sent_and_summed(array, axis, dim):
    peers = lax.axis_size(axis)
    tiles = lax.all_to_all(split_up(array, dim, peers), axis, 0, 0, tiled=True)
    return jnp.sum(tiles.astype(jnp.float32), axis=0)


def by_axis(array, axes):
    for axis in axes:
        array = lax.psum(array, axis)
    return array


def silu_slope(values):
    sigmoid_value = jax.nn.sigmoid(values)
    return sigmoid_value * (1.0 + values * (1.0 - sigmoid_value))


def product(form, left, right):
    return jnp.einsum(form, left, right, preferred_element_type=jnp.float32)


def dequantize(stored, scales):
    user_count, row_count, model_width = stored.shape
    block_count, head_count = (scales.shape[1], scales.shape[2])
    shaped = stored.astype(jnp.float32).reshape(
        user_count, block_count, row_count // block_count, head_count, model_width // head_count
    )
    scaled = shaped * scales[:, :, None, :, None]
    return scaled.astype(jnp.bfloat16).reshape(user_count * row_count, model_width)


def key_mask(user_ids, lengths, shard_index, hist_rows, span_rows):
    query_count = user_ids.shape[0]
    user_count = lengths.shape[0]
    key_index = jnp.arange(user_count * hist_rows, dtype=jnp.int32)
    key_user = key_index // hist_rows
    key_row = shard_index * hist_rows + key_index % hist_rows
    user_range = jnp.arange(user_count, dtype=jnp.int32)
    key_limit = jnp.sum(
        jnp.where(key_user[:, None] == user_range[None, :], lengths[None, :], 0), axis=1
    )
    history_mask = (user_ids[:, None] == key_user[None, :]) & (key_row < key_limit)[None, :]
    span_start = shard_index * span_rows
    span_pos = span_start + jnp.arange(span_rows, dtype=jnp.int32)
    span_users = lax.dynamic_slice_in_dim(user_ids, span_start, span_rows, 0)
    query_pos = jnp.arange(query_count, dtype=jnp.int32)
    span_mask = (user_ids[:, None] == span_users[None, :]) & (
        span_pos[None, :] <= query_pos[:, None]
    )
    return jnp.concatenate([history_mask, span_mask], axis=1)


def split_heads(matrix, head_count):
    return matrix.reshape(matrix.shape[0], head_count, matrix.shape[1] // head_count)


def forward_part(queries, keys, values_all, mask, head_count):
    head_size = queries.shape[1] // head_count
    scores = product(
        "qhd,khd->hqk", split_heads(queries, head_count), split_heads(keys, head_count)
    ) / math.sqrt(head_size)
    attn = jnp.where(mask[None], jax.nn.silu(scores), 0.0).astype(jnp.bfloat16)
    mixed = product("hqk,khd->qhd", attn, split_heads(values_all, head_count))
    weighted_slope = jnp.where(mask[None], silu_slope(scores), 0.0) / math.sqrt(head_size)
    return (mixed.reshape(queries.shape[0], queries.shape[1]), weighted_slope)


def backward_part(keys, values_all, weighted_slope, mixed_grad, head_count):
    attn_grad = product(
        "qhd,khd->hqk", split_heads(mixed_grad, head_count), split_heads(values_all, head_count)
    )
    score_grad = (attn_grad * weighted_slope).astype(jnp.bfloat16)
    query_grad = product("hqk,khd->qhd", score_grad, split_heads(keys, head_count))
    return query_grad.reshape(mixed_grad.shape[0], mixed_grad.shape[1])


def shards(
    tokens,
    gate_values,
    output_grad,
    query_weight,
    master,
    moment,
    second,
    key_codes,
    value_codes,
    key_scales,
    value_scales,
    span_keys,
    span_values,
    lengths,
    segments,
):
    model_width = query_weight.shape[0]
    shard_index = lax.axis_index(CACHE)
    features = collect_cache(tokens, 1)
    query_pre = jnp.dot(features, query_weight, preferred_element_type=jnp.float32) / math.sqrt(
        model_width
    )
    query_block = jax.nn.silu(query_pre).astype(jnp.bfloat16)
    queries = collect_cache(query_block, 1)
    user_ids = segments[0]
    hist_rows = key_codes.shape[1]
    span_rows = span_keys.shape[0]
    keys = jnp.concatenate([dequantize(key_codes, key_scales), span_keys], axis=0)
    values_all = jnp.concatenate([dequantize(value_codes, value_scales), span_values], axis=0)
    mask = key_mask(user_ids, lengths, shard_index, hist_rows, span_rows)
    mixed_part, weighted_slope = forward_part(queries, keys, values_all, mask, HEADS)
    gate_float = gate_values.astype(jnp.float32)
    mixed_block = summed_over_cache(mixed_part, 1)
    back = output_grad.astype(jnp.float32) * gate_float
    row_sum, row_square, back_sum, back_mixed = packed_total(
        (
            jnp.sum(mixed_block, axis=1),
            jnp.sum(mixed_block * mixed_block, axis=1),
            jnp.sum(back, axis=1),
            jnp.sum(back * mixed_block, axis=1),
        ),
        CACHE,
    )
    row_mean = (row_sum / model_width)[:, None]
    row_var = (row_square / model_width)[:, None] - row_mean * row_mean
    inverse = 1.0 / jnp.sqrt(row_var + 1e-05)
    normed = (mixed_block - row_mean) * inverse
    layer_block = (gate_float * normed).astype(jnp.bfloat16)
    back_cross = inverse[:, 0] * (back_mixed - row_mean[:, 0] * back_sum)
    grad_block = inverse * (
        back - (back_sum / model_width)[:, None] - normed * (back_cross / model_width)[:, None]
    )
    mixed_grad = collect_cache(grad_block.astype(jnp.bfloat16), 1)
    query_part = backward_part(keys, values_all, weighted_slope, mixed_grad, HEADS)
    query_grad = rounded_sum_over_cache(query_part, 1)
    pre_grad = (query_grad * silu_slope(query_pre)).astype(jnp.bfloat16)
    weight_part = lax.dot_general(
        features, pre_grad, (((0,), (0,)), ((), ())), preferred_element_type=jnp.float32
    ) / math.sqrt(model_width)
    grad_owned = sent_and_summed(weight_part.astype(jnp.bfloat16), DP, 0)
    square_total = of_everyone(jnp.sum(grad_owned * grad_owned).reshape(1), CACHE_DP)[0]
    grad_level = jnp.sqrt(square_total / (model_width * model_width))
    clip_factor = jnp.minimum(1.0, 0.5 / (grad_level + 1e-06))
    clipped = clip_factor * grad_owned
    new_moment = 0.9 * moment + 0.1 * clipped
    new_second = 0.95 * second + 0.05 * clipped * clipped
    first_fix = new_moment / (1.0 - 0.9**STEP)
    second_fix = new_second / (1.0 - 0.95**STEP)
    new_master = master - 0.01 * (first_fix / (jnp.sqrt(second_fix) + 1e-08) + 0.1 * master)
    new_weight = collect(new_master.astype(jnp.bfloat16), DP, 0)
    return (layer_block, new_weight, new_master, new_moment, new_second)


def solution(mesh):
    torus = Mesh(
        mesh.devices.reshape(2, 8, 2, 8, 2), ("cache_0", "cache_1", "cache_2", "dp_0", "dp_1")
    )
    placed = (
        P(DP, CACHE),
        P(DP, CACHE),
        P(DP, CACHE),
        P(None, CACHE),
        P(DP, CACHE),
        P(DP, CACHE),
        P(DP, CACHE),
        P(DP, CACHE, None),
        P(DP, CACHE, None),
        P(DP, CACHE, None),
        P(DP, CACHE, None),
        P(DP_CACHE, None),
        P(DP_CACHE, None),
        P(DP),
        P(DP, None),
    )
    return jax.shard_map(
        shards,
        mesh=torus,
        in_specs=placed,
        out_specs=(P(DP, CACHE), P(None, CACHE), P(DP, CACHE), P(DP, CACHE), P(DP, CACHE)),
        check_vma=False,
    )
```

```python
import math

import jax
import jax.numpy as jnp
from jax import lax
from jax.sharding import Mesh
from jax.sharding import PartitionSpec as P

HEADS = 16
STEP = 20
CACHE = ("cache_0", "cache_1", "cache_2")
DP = ("dp_0", "dp_1")
CACHE_DP = ("cache_0", "cache_1", "cache_2", "dp_0", "dp_1")
DP_CACHE = ("dp_0", "dp_1", "cache_0", "cache_1", "cache_2")


def split_up(array, dim, peers):
    dims = array.shape
    tiles = array.reshape(*dims[:dim], peers, dims[dim] // peers, *dims[dim + 1 :])
    return jnp.moveaxis(tiles, dim, 0)


def summed_on_arrival(array, axis, dim):
    tiles = split_up(array, dim, lax.axis_size(axis))
    arrived = lax.all_to_all(tiles, axis, split_axis=0, concat_axis=0, tiled=True)
    return arrived.sum(axis=0)


def sent_to_all(array, axis):
    copies = jnp.broadcast_to(array, (lax.axis_size(axis), *array.shape))
    return lax.all_to_all(copies, axis, split_axis=0, concat_axis=0, tiled=True)


def of_everyone(array, axis):
    everything = sent_to_all(array, axis)
    return jnp.sum(everything, axis=0)


def packed_total(arrays, axis):
    flat, at, outs = (jnp.concatenate([a.reshape(-1) for a in arrays]), 0, [])
    subtotal = of_everyone(flat, axis)
    for a in arrays:
        outs.append(subtotal[at : at + a.size].reshape(a.shape))
        at += a.size
    return tuple(outs)


def in_order(tiles, dim):
    dims = list(tiles.shape[1:])
    dims[dim] *= tiles.shape[0]
    return jnp.moveaxis(tiles, 0, dim).reshape(dims)


CHIPS = ("cache_0", "cache_1")
CORE = "cache_2"


def collect_cache(array, dim):
    chips = lax.axis_size(CHIPS)
    across = lax.all_to_all(
        jnp.broadcast_to(array, (chips, *array.shape)), CHIPS, 0, 0, tiled=True
    )
    cores = lax.axis_size(CORE)
    pairs = lax.all_to_all(
        jnp.broadcast_to(across, (cores, *across.shape)), CORE, 0, 0, tiled=True
    )
    tiles = jnp.swapaxes(pairs, 0, 1).reshape(chips * cores, *array.shape)
    return in_order(tiles, dim)


def summed_over_cache(array, dim):
    chips, cores = (lax.axis_size(CHIPS), lax.axis_size(CORE))
    tiles = split_up(array, dim, chips * cores)
    tiles = jnp.swapaxes(tiles.reshape(chips, cores, *tiles.shape[1:]), 0, 1)
    on_chip = lax.all_to_all(tiles, CORE, 0, 0, tiled=True).sum(axis=0)
    return lax.all_to_all(on_chip, CHIPS, 0, 0, tiled=True).sum(axis=0)


def rounded_sum_over_cache(array, dim):
    chips, cores = (lax.axis_size(CHIPS), lax.axis_size(CORE))
    tiles = split_up(array.astype(jnp.bfloat16), dim, chips * cores)
    tiles = jnp.swapaxes(tiles.reshape(chips, cores, *tiles.shape[1:]), 0, 1)
    on_chip = lax.all_to_all(tiles, CORE, 0, 0, tiled=True)
    pair_sum = jnp.sum(on_chip.astype(jnp.float32), axis=0).astype(jnp.bfloat16)
    arrived = lax.all_to_all(pair_sum, CHIPS, 0, 0, tiled=True)
    return jnp.sum(arrived.astype(jnp.float32), axis=0)


def tokens_and_rows(tokens, gate_values, output_grad):
    chips, cores = (lax.axis_size(CHIPS), lax.axis_size(CORE))
    peers = chips * cores
    rows, cols = tokens.shape
    row_block = rows // peers
    flat = rows * cols
    pair = jnp.stack([gate_values, output_grad])
    by_chip = pair.reshape(2, chips, cores * row_block, cols).transpose(1, 0, 2, 3)
    outgoing = jnp.concatenate(
        [jnp.broadcast_to(tokens.reshape(1, flat), (chips, flat)), by_chip.reshape(chips, -1)], axis=1
    )
    across = lax.all_to_all(outgoing, CHIPS, 0, 0, tiled=True)
    token_tiles = across[:, :flat]
    row_tiles = across[:, flat:].reshape(chips, 2, cores, row_block, cols)
    outgoing = jnp.concatenate(
        [
            jnp.broadcast_to(token_tiles[None], (cores, chips, flat)),
            row_tiles.transpose(2, 0, 1, 3, 4).reshape(cores, chips, 2 * row_block * cols),
        ],
        axis=2,
    )
    arrived = jnp.swapaxes(lax.all_to_all(outgoing, CORE, 0, 0, tiled=True), 0, 1)
    arrived = arrived.reshape(peers, -1)
    features = in_order(arrived[:, :flat].reshape(peers, rows, cols), 1)
    own_rows = arrived[:, flat:].reshape(peers, 2, row_block, cols).transpose(1, 2, 0, 3)
    own_rows = own_rows.reshape(2, row_block, peers * cols)
    return features, own_rows[0], own_rows[1]


def rows_summed_over_cache(array):
    chips, cores = (lax.axis_size(CHIPS), lax.axis_size(CORE))
    tiles = array.reshape(chips, cores, array.shape[0] // (chips * cores), array.shape[1])
    on_chip = lax.all_to_all(jnp.swapaxes(tiles, 0, 1), CORE, 0, 0, tiled=True).sum(axis=0)
    return lax.all_to_all(on_chip, CHIPS, 0, 0, tiled=True).sum(axis=0)


def rows_to_everyone(grad_rows, layer_rows):
    chips, cores = (lax.axis_size(CHIPS), lax.axis_size(CORE))
    peers = chips * cores
    row_block, width = grad_rows.shape
    cols = width // peers
    flat = row_block * width
    layer_by_chip = layer_rows.reshape(row_block, chips, cores * cols).transpose(1, 0, 2)
    outgoing = jnp.concatenate(
        [
            jnp.broadcast_to(grad_rows.reshape(1, flat), (chips, flat)),
            layer_by_chip.reshape(chips, -1),
        ],
        axis=1,
    )
    across = lax.all_to_all(outgoing, CHIPS, 0, 0, tiled=True)
    grad_tiles = across[:, :flat]
    layer_tiles = across[:, flat:].reshape(chips, row_block, cores, cols)
    outgoing = jnp.concatenate(
        [
            jnp.broadcast_to(grad_tiles[None], (cores, chips, flat)),
            layer_tiles.transpose(2, 0, 1, 3).reshape(cores, chips, row_block * cols),
        ],
        axis=2,
    )
    arrived = jnp.swapaxes(lax.all_to_all(outgoing, CORE, 0, 0, tiled=True), 0, 1)
    arrived = arrived.reshape(peers, -1)
    mixed_grad = arrived[:, :flat].reshape(peers * row_block, width)
    layer_block = arrived[:, flat:].reshape(peers * row_block, cols)
    return mixed_grad, layer_block


def collect(array, axis, dim):
    tiles = sent_to_all(array, axis)
    return in_order(tiles, dim)


def sent_and_summed(array, axis, dim):
    peers = lax.axis_size(axis)
    tiles = lax.all_to_all(split_up(array, dim, peers), axis, 0, 0, tiled=True)
    return jnp.sum(tiles.astype(jnp.float32), axis=0)


def by_axis(array, axes):
    for axis in axes:
        array = lax.psum(array, axis)
    return array


def silu_slope(values):
    sigmoid_value = jax.nn.sigmoid(values)
    return sigmoid_value * (1.0 + values * (1.0 - sigmoid_value))


def product(form, left, right):
    return jnp.einsum(form, left, right, preferred_element_type=jnp.float32)


def dequantize(stored, scales):
    user_count, row_count, model_width = stored.shape
    block_count, head_count = (scales.shape[1], scales.shape[2])
    shaped = stored.astype(jnp.float32).reshape(
        user_count, block_count, row_count // block_count, head_count, model_width // head_count
    )
    scaled = shaped * scales[:, :, None, :, None]
    return scaled.astype(jnp.bfloat16).reshape(user_count * row_count, model_width)


def key_mask(user_ids, lengths, shard_index, hist_rows, span_rows):
    query_count = user_ids.shape[0]
    user_count = lengths.shape[0]
    key_index = jnp.arange(user_count * hist_rows, dtype=jnp.int32)
    key_user = key_index // hist_rows
    key_row = shard_index * hist_rows + key_index % hist_rows
    user_range = jnp.arange(user_count, dtype=jnp.int32)
    key_limit = jnp.sum(
        jnp.where(key_user[:, None] == user_range[None, :], lengths[None, :], 0), axis=1
    )
    history_mask = (user_ids[:, None] == key_user[None, :]) & (key_row < key_limit)[None, :]
    span_start = shard_index * span_rows
    span_pos = span_start + jnp.arange(span_rows, dtype=jnp.int32)
    span_users = lax.dynamic_slice_in_dim(user_ids, span_start, span_rows, 0)
    query_pos = jnp.arange(query_count, dtype=jnp.int32)
    span_mask = (user_ids[:, None] == span_users[None, :]) & (
        span_pos[None, :] <= query_pos[:, None]
    )
    return jnp.concatenate([history_mask, span_mask], axis=1)


def split_heads(matrix, head_count):
    return matrix.reshape(matrix.shape[0], head_count, matrix.shape[1] // head_count)


def forward_part(queries, keys, values_all, mask, head_count):
    head_size = queries.shape[1] // head_count
    scores = product(
        "qhd,khd->hqk", split_heads(queries, head_count), split_heads(keys, head_count)
    ) / math.sqrt(head_size)
    attn = jnp.where(mask[None], jax.nn.silu(scores), 0.0).astype(jnp.bfloat16)
    mixed = product("hqk,khd->qhd", attn, split_heads(values_all, head_count))
    weighted_slope = jnp.where(mask[None], silu_slope(scores), 0.0) / math.sqrt(head_size)
    return (mixed.reshape(queries.shape[0], queries.shape[1]), weighted_slope)


def backward_part(keys, values_all, weighted_slope, mixed_grad, head_count):
    attn_grad = product(
        "qhd,khd->hqk", split_heads(mixed_grad, head_count), split_heads(values_all, head_count)
    )
    score_grad = (attn_grad * weighted_slope).astype(jnp.bfloat16)
    query_grad = product("hqk,khd->qhd", score_grad, split_heads(keys, head_count))
    return query_grad.reshape(mixed_grad.shape[0], mixed_grad.shape[1])


def shards(
    tokens,
    gate_values,
    output_grad,
    query_weight,
    master,
    moment,
    second,
    key_codes,
    value_codes,
    key_scales,
    value_scales,
    span_keys,
    span_values,
    lengths,
    segments,
):
    model_width = query_weight.shape[0]
    shard_index = lax.axis_index(CACHE)
    features, gate_rows, grad_rows_in = tokens_and_rows(tokens, gate_values, output_grad)
    query_pre = jnp.dot(features, query_weight, preferred_element_type=jnp.float32) / math.sqrt(
        model_width
    )
    query_block = jax.nn.silu(query_pre).astype(jnp.bfloat16)
    queries = collect_cache(query_block, 1)
    user_ids = segments[0]
    hist_rows = key_codes.shape[1]
    span_rows = span_keys.shape[0]
    keys = jnp.concatenate([dequantize(key_codes, key_scales), span_keys], axis=0)
    values_all = jnp.concatenate([dequantize(value_codes, value_scales), span_values], axis=0)
    mask = key_mask(user_ids, lengths, shard_index, hist_rows, span_rows)
    mixed_part, weighted_slope = forward_part(queries, keys, values_all, mask, HEADS)
    mixed_rows = rows_summed_over_cache(mixed_part)
    row_mean = jnp.mean(mixed_rows, axis=1, keepdims=True)
    centered = mixed_rows - row_mean
    row_var = jnp.mean(centered * centered, axis=1, keepdims=True)
    inverse = 1.0 / jnp.sqrt(row_var + 1e-05)
    normed = centered * inverse
    gate_float = gate_rows.astype(jnp.float32)
    layer_rows = (gate_float * normed).astype(jnp.bfloat16)
    back = grad_rows_in.astype(jnp.float32) * gate_float
    grad_rows = inverse * (
        back
        - jnp.mean(back, axis=1, keepdims=True)
        - normed * jnp.mean(back * normed, axis=1, keepdims=True)
    )
    mixed_grad, layer_block = rows_to_everyone(grad_rows.astype(jnp.bfloat16), layer_rows)
    query_part = backward_part(keys, values_all, weighted_slope, mixed_grad, HEADS)
    query_grad = rounded_sum_over_cache(query_part, 1)
    pre_grad = (query_grad * silu_slope(query_pre)).astype(jnp.bfloat16)
    weight_part = lax.dot_general(
        features, pre_grad, (((0,), (0,)), ((), ())), preferred_element_type=jnp.float32
    ) / math.sqrt(model_width)
    grad_owned = sent_and_summed(weight_part.astype(jnp.bfloat16), DP, 0)
    square_total = of_everyone(jnp.sum(grad_owned * grad_owned).reshape(1), CACHE_DP)[0]
    grad_level = jnp.sqrt(square_total / (model_width * model_width))
    clip_factor = jnp.minimum(1.0, 0.5 / (grad_level + 1e-06))
    clipped = clip_factor * grad_owned
    new_moment = 0.9 * moment + 0.1 * clipped
    new_second = 0.95 * second + 0.05 * clipped * clipped
    first_fix = new_moment / (1.0 - 0.9**STEP)
    second_fix = new_second / (1.0 - 0.95**STEP)
    new_master = master - 0.01 * (first_fix / (jnp.sqrt(second_fix) + 1e-08) + 0.1 * master)
    new_weight = collect(new_master.astype(jnp.bfloat16), DP, 0)
    return (layer_block, new_weight, new_master, new_moment, new_second)


def solution(mesh):
    torus = Mesh(
        mesh.devices.reshape(2, 8, 2, 8, 2), ("cache_0", "cache_1", "cache_2", "dp_0", "dp_1")
    )
    placed = (
        P(DP, CACHE),
        P(DP, CACHE),
        P(DP, CACHE),
        P(None, CACHE),
        P(DP, CACHE),
        P(DP, CACHE),
        P(DP, CACHE),
        P(DP, CACHE, None),
        P(DP, CACHE, None),
        P(DP, CACHE, None),
        P(DP, CACHE, None),
        P(DP_CACHE, None),
        P(DP_CACHE, None),
        P(DP),
        P(DP, None),
    )
    return jax.shard_map(
        shards,
        mesh=torus,
        in_specs=placed,
        out_specs=(P(DP, CACHE), P(None, CACHE), P(DP, CACHE), P(DP, CACHE), P(DP, CACHE)),
        check_vma=False,
    )
```

```python
import math

import jax
import jax.numpy as jnp
from jax import lax
from jax.sharding import Mesh
from jax.sharding import PartitionSpec as P

HEADS = 16
STEP = 20
CACHE = ("cache_0", "cache_1", "cache_2")
DP = ("dp_0", "dp_1")
CACHE_DP = ("cache_0", "cache_1", "cache_2", "dp_0", "dp_1")
DP_CACHE = ("dp_0", "dp_1", "cache_0", "cache_1", "cache_2")


def split_up(array, dim, peers):
    dims = array.shape
    tiles = array.reshape(*dims[:dim], peers, dims[dim] // peers, *dims[dim + 1 :])
    return jnp.moveaxis(tiles, dim, 0)


def summed_on_arrival(array, axis, dim):
    tiles = split_up(array, dim, lax.axis_size(axis))
    arrived = lax.all_to_all(tiles, axis, split_axis=0, concat_axis=0, tiled=True)
    return arrived.sum(axis=0)


def sent_to_all(array, axis):
    copies = jnp.broadcast_to(array, (lax.axis_size(axis), *array.shape))
    return lax.all_to_all(copies, axis, split_axis=0, concat_axis=0, tiled=True)


def of_everyone(array, axis):
    everything = sent_to_all(array, axis)
    return jnp.sum(everything, axis=0)


def packed_total(arrays, axis):
    flat, at, outs = (jnp.concatenate([a.reshape(-1) for a in arrays]), 0, [])
    subtotal = of_everyone(flat, axis)
    for a in arrays:
        outs.append(subtotal[at : at + a.size].reshape(a.shape))
        at += a.size
    return tuple(outs)


def in_order(tiles, dim):
    dims = list(tiles.shape[1:])
    dims[dim] *= tiles.shape[0]
    return jnp.moveaxis(tiles, 0, dim).reshape(dims)


CHIPS = ("cache_0", "cache_1")
CORE = "cache_2"


def collect_cache(array, dim):
    chips = lax.axis_size(CHIPS)
    across = lax.all_to_all(
        jnp.broadcast_to(array, (chips, *array.shape)), CHIPS, 0, 0, tiled=True
    )
    cores = lax.axis_size(CORE)
    pairs = lax.all_to_all(
        jnp.broadcast_to(across, (cores, *across.shape)), CORE, 0, 0, tiled=True
    )
    tiles = jnp.swapaxes(pairs, 0, 1).reshape(chips * cores, *array.shape)
    return in_order(tiles, dim)


def summed_over_cache(array, dim):
    chips, cores = (lax.axis_size(CHIPS), lax.axis_size(CORE))
    tiles = split_up(array, dim, chips * cores)
    tiles = jnp.swapaxes(tiles.reshape(chips, cores, *tiles.shape[1:]), 0, 1)
    on_chip = lax.all_to_all(tiles, CORE, 0, 0, tiled=True).sum(axis=0)
    return lax.all_to_all(on_chip, CHIPS, 0, 0, tiled=True).sum(axis=0)


def rounded_sum_over_cache(array, dim):
    chips, cores = (lax.axis_size(CHIPS), lax.axis_size(CORE))
    tiles = split_up(array.astype(jnp.bfloat16), dim, chips * cores)
    tiles = jnp.swapaxes(tiles.reshape(chips, cores, *tiles.shape[1:]), 0, 1)
    on_chip = lax.all_to_all(tiles, CORE, 0, 0, tiled=True)
    pair_sum = jnp.sum(on_chip.astype(jnp.float32), axis=0).astype(jnp.bfloat16)
    arrived = lax.all_to_all(pair_sum, CHIPS, 0, 0, tiled=True)
    return jnp.sum(arrived.astype(jnp.float32), axis=0)


def rows_summed_over_cache(array):
    chips, cores = (lax.axis_size(CHIPS), lax.axis_size(CORE))
    tiles = array.reshape(chips, cores, array.shape[0] // (chips * cores), array.shape[1])
    on_chip = lax.all_to_all(jnp.swapaxes(tiles, 0, 1), CORE, 0, 0, tiled=True).sum(axis=0)
    return lax.all_to_all(on_chip, CHIPS, 0, 0, tiled=True).sum(axis=0)


def columns_to_rows(array):
    peers = lax.axis_size(CACHE)
    lead, rows, cols = array.shape
    tiles = array.reshape(lead, peers, rows // peers, cols).transpose(1, 0, 2, 3)
    arrived = lax.all_to_all(tiles, CACHE, 0, 0, tiled=True)
    return arrived.transpose(1, 2, 0, 3).reshape(lead, rows // peers, peers * cols)


def rows_to_columns(array):
    peers = lax.axis_size(CACHE)
    rows, width = array.shape
    tiles = array.reshape(rows, peers, width // peers).transpose(1, 0, 2)
    arrived = lax.all_to_all(tiles, CACHE, 0, 0, tiled=True)
    return arrived.reshape(peers * rows, width // peers)


def collect(array, axis, dim):
    tiles = sent_to_all(array, axis)
    return in_order(tiles, dim)


def sent_and_summed(array, axis, dim):
    peers = lax.axis_size(axis)
    tiles = lax.all_to_all(split_up(array, dim, peers), axis, 0, 0, tiled=True)
    return jnp.sum(tiles.astype(jnp.float32), axis=0)


def by_axis(array, axes):
    for axis in axes:
        array = lax.psum(array, axis)
    return array


def silu_slope(values):
    sigmoid_value = jax.nn.sigmoid(values)
    return sigmoid_value * (1.0 + values * (1.0 - sigmoid_value))


def product(form, left, right):
    return jnp.einsum(form, left, right, preferred_element_type=jnp.float32)


def dequantize(stored, scales):
    user_count, row_count, model_width = stored.shape
    block_count, head_count = (scales.shape[1], scales.shape[2])
    shaped = stored.astype(jnp.float32).reshape(
        user_count, block_count, row_count // block_count, head_count, model_width // head_count
    )
    scaled = shaped * scales[:, :, None, :, None]
    return scaled.astype(jnp.bfloat16).reshape(user_count * row_count, model_width)


def key_mask(user_ids, lengths, shard_index, hist_rows, span_rows):
    query_count = user_ids.shape[0]
    user_count = lengths.shape[0]
    key_index = jnp.arange(user_count * hist_rows, dtype=jnp.int32)
    key_user = key_index // hist_rows
    key_row = shard_index * hist_rows + key_index % hist_rows
    user_range = jnp.arange(user_count, dtype=jnp.int32)
    key_limit = jnp.sum(
        jnp.where(key_user[:, None] == user_range[None, :], lengths[None, :], 0), axis=1
    )
    history_mask = (user_ids[:, None] == key_user[None, :]) & (key_row < key_limit)[None, :]
    span_start = shard_index * span_rows
    span_pos = span_start + jnp.arange(span_rows, dtype=jnp.int32)
    span_users = lax.dynamic_slice_in_dim(user_ids, span_start, span_rows, 0)
    query_pos = jnp.arange(query_count, dtype=jnp.int32)
    span_mask = (user_ids[:, None] == span_users[None, :]) & (
        span_pos[None, :] <= query_pos[:, None]
    )
    return jnp.concatenate([history_mask, span_mask], axis=1)


def split_heads(matrix, head_count):
    return matrix.reshape(matrix.shape[0], head_count, matrix.shape[1] // head_count)


def forward_part(queries, keys, values_all, mask, head_count):
    head_size = queries.shape[1] // head_count
    scores = product(
        "qhd,khd->hqk", split_heads(queries, head_count), split_heads(keys, head_count)
    ) / math.sqrt(head_size)
    attn = jnp.where(mask[None], jax.nn.silu(scores), 0.0).astype(jnp.bfloat16)
    mixed = product("hqk,khd->qhd", attn, split_heads(values_all, head_count))
    weighted_slope = jnp.where(mask[None], silu_slope(scores), 0.0) / math.sqrt(head_size)
    return (mixed.reshape(queries.shape[0], queries.shape[1]), weighted_slope)


def backward_part(keys, values_all, weighted_slope, mixed_grad, head_count):
    attn_grad = product(
        "qhd,khd->hqk", split_heads(mixed_grad, head_count), split_heads(values_all, head_count)
    )
    score_grad = (attn_grad * weighted_slope).astype(jnp.bfloat16)
    query_grad = product("hqk,khd->qhd", score_grad, split_heads(keys, head_count))
    return query_grad.reshape(mixed_grad.shape[0], mixed_grad.shape[1])


def shards(
    tokens,
    gate_values,
    output_grad,
    query_weight,
    master,
    moment,
    second,
    key_codes,
    value_codes,
    key_scales,
    value_scales,
    span_keys,
    span_values,
    lengths,
    segments,
):
    model_width = query_weight.shape[0]
    shard_index = lax.axis_index(CACHE)
    features = collect_cache(tokens, 1)
    gate_rows, grad_rows_in = columns_to_rows(jnp.stack([gate_values, output_grad]))
    query_pre = jnp.dot(features, query_weight, preferred_element_type=jnp.float32) / math.sqrt(
        model_width
    )
    query_block = jax.nn.silu(query_pre).astype(jnp.bfloat16)
    query_block, gate_rows, grad_rows_in = lax.optimization_barrier(
        (query_block, gate_rows, grad_rows_in)
    )
    queries = collect_cache(query_block, 1)
    user_ids = segments[0]
    hist_rows = key_codes.shape[1]
    span_rows = span_keys.shape[0]
    keys = jnp.concatenate([dequantize(key_codes, key_scales), span_keys], axis=0)
    values_all = jnp.concatenate([dequantize(value_codes, value_scales), span_values], axis=0)
    mask = key_mask(user_ids, lengths, shard_index, hist_rows, span_rows)
    mixed_part, weighted_slope = forward_part(queries, keys, values_all, mask, HEADS)
    mixed_rows = rows_summed_over_cache(mixed_part)
    row_mean = jnp.mean(mixed_rows, axis=1, keepdims=True)
    centered = mixed_rows - row_mean
    row_var = jnp.mean(centered * centered, axis=1, keepdims=True)
    inverse = 1.0 / jnp.sqrt(row_var + 1e-05)
    normed = centered * inverse
    gate_float = gate_rows.astype(jnp.float32)
    layer_block = rows_to_columns((gate_float * normed).astype(jnp.bfloat16))
    back = grad_rows_in.astype(jnp.float32) * gate_float
    grad_rows = inverse * (
        back
        - jnp.mean(back, axis=1, keepdims=True)
        - normed * jnp.mean(back * normed, axis=1, keepdims=True)
    )
    mixed_grad = collect_cache(grad_rows.astype(jnp.bfloat16), 0)
    query_part = backward_part(keys, values_all, weighted_slope, mixed_grad, HEADS)
    query_grad = rounded_sum_over_cache(query_part, 1)
    pre_grad = (query_grad * silu_slope(query_pre)).astype(jnp.bfloat16)
    weight_part = lax.dot_general(
        features, pre_grad, (((0,), (0,)), ((), ())), preferred_element_type=jnp.float32
    ) / math.sqrt(model_width)
    grad_owned = sent_and_summed(weight_part.astype(jnp.bfloat16), DP, 0)
    square_total = of_everyone(jnp.sum(grad_owned * grad_owned).reshape(1), CACHE_DP)[0]
    grad_level = jnp.sqrt(square_total / (model_width * model_width))
    clip_factor = jnp.minimum(1.0, 0.5 / (grad_level + 1e-06))
    clipped = clip_factor * grad_owned
    new_moment = 0.9 * moment + 0.1 * clipped
    new_second = 0.95 * second + 0.05 * clipped * clipped
    first_fix = new_moment / (1.0 - 0.9**STEP)
    second_fix = new_second / (1.0 - 0.95**STEP)
    new_master = master - 0.01 * (first_fix / (jnp.sqrt(second_fix) + 1e-08) + 0.1 * master)
    new_weight = collect(new_master.astype(jnp.bfloat16), DP, 0)
    return (layer_block, new_weight, new_master, new_moment, new_second)


def solution(mesh):
    torus = Mesh(
        mesh.devices.reshape(2, 8, 2, 8, 2), ("cache_0", "cache_1", "cache_2", "dp_0", "dp_1")
    )
    placed = (
        P(DP, CACHE),
        P(DP, CACHE),
        P(DP, CACHE),
        P(None, CACHE),
        P(DP, CACHE),
        P(DP, CACHE),
        P(DP, CACHE),
        P(DP, CACHE, None),
        P(DP, CACHE, None),
        P(DP, CACHE, None),
        P(DP, CACHE, None),
        P(DP_CACHE, None),
        P(DP_CACHE, None),
        P(DP),
        P(DP, None),
    )
    return jax.shard_map(
        shards,
        mesh=torus,
        in_specs=placed,
        out_specs=(P(DP, CACHE), P(None, CACHE), P(DP, CACHE), P(DP, CACHE), P(DP, CACHE)),
        check_vma=False,
    )
```

```python
import math

import jax
import jax.numpy as jnp
from jax import lax
from jax.sharding import Mesh
from jax.sharding import PartitionSpec as P

HEADS = 16
STEP = 20
CACHE = ("cache_0", "cache_1", "cache_2")
DP = ("dp_0", "dp_1")
CACHE_DP = ("cache_0", "cache_1", "cache_2", "dp_0", "dp_1")
DP_CACHE = ("dp_0", "dp_1", "cache_0", "cache_1", "cache_2")


def split_up(array, dim, peers):
    dims = array.shape
    tiles = array.reshape(*dims[:dim], peers, dims[dim] // peers, *dims[dim + 1 :])
    return jnp.moveaxis(tiles, dim, 0)


def summed_on_arrival(array, axis, dim):
    tiles = split_up(array, dim, lax.axis_size(axis))
    arrived = lax.all_to_all(tiles, axis, split_axis=0, concat_axis=0, tiled=True)
    return arrived.sum(axis=0)


def sent_to_all(array, axis):
    copies = jnp.broadcast_to(array, (lax.axis_size(axis), *array.shape))
    return lax.all_to_all(copies, axis, split_axis=0, concat_axis=0, tiled=True)


def of_everyone(array, axis):
    everything = sent_to_all(array, axis)
    return jnp.sum(everything, axis=0)


def packed_total(arrays, axis):
    flat, at, outs = (jnp.concatenate([a.reshape(-1) for a in arrays]), 0, [])
    subtotal = of_everyone(flat, axis)
    for a in arrays:
        outs.append(subtotal[at : at + a.size].reshape(a.shape))
        at += a.size
    return tuple(outs)


def in_order(tiles, dim):
    dims = list(tiles.shape[1:])
    dims[dim] *= tiles.shape[0]
    return jnp.moveaxis(tiles, 0, dim).reshape(dims)


CHIPS = ("cache_0", "cache_1")
CORE = "cache_2"


def partner(array):
    return lax.ppermute(array, CORE, [(0, 1), (1, 0)])


def by_core(tiles):
    first = lax.axis_index(CORE) == 0
    return (jnp.where(first, tiles[0], tiles[1]), jnp.where(first, tiles[1], tiles[0]))


def collect_cache(array, dim):
    chips = lax.axis_size(CHIPS)
    across = lax.all_to_all(
        jnp.broadcast_to(array, (chips, *array.shape)), CHIPS, 0, 0, tiled=True
    )
    other = partner(across)
    first = lax.axis_index(CORE) == 0
    pairs = jnp.stack([jnp.where(first, across, other), jnp.where(first, other, across)])
    tiles = jnp.swapaxes(pairs, 0, 1).reshape(2 * chips, *array.shape)
    return in_order(tiles, dim)


def summed_over_cache(array, dim):
    chips, cores = (lax.axis_size(CHIPS), lax.axis_size(CORE))
    tiles = split_up(array, dim, chips * cores)
    tiles = jnp.swapaxes(tiles.reshape(chips, cores, *tiles.shape[1:]), 0, 1)
    kept, sent = by_core(tiles)
    on_chip = kept + partner(sent)
    return lax.all_to_all(on_chip, CHIPS, 0, 0, tiled=True).sum(axis=0)


def rounded_sum_over_cache(array, dim):
    chips, cores = (lax.axis_size(CHIPS), lax.axis_size(CORE))
    tiles = split_up(array.astype(jnp.bfloat16), dim, chips * cores)
    tiles = jnp.swapaxes(tiles.reshape(chips, cores, *tiles.shape[1:]), 0, 1)
    kept, sent = by_core(tiles)
    pair_sum = kept.astype(jnp.float32) + partner(sent).astype(jnp.float32)
    arrived = lax.all_to_all(pair_sum.astype(jnp.bfloat16), CHIPS, 0, 0, tiled=True)
    return jnp.sum(arrived.astype(jnp.float32), axis=0)


def collect(array, axis, dim):
    tiles = sent_to_all(array, axis)
    return in_order(tiles, dim)


def sent_and_summed(array, axis, dim):
    peers = lax.axis_size(axis)
    tiles = lax.all_to_all(split_up(array, dim, peers), axis, 0, 0, tiled=True)
    return jnp.sum(tiles.astype(jnp.float32), axis=0)


def by_axis(array, axes):
    for axis in axes:
        array = lax.psum(array, axis)
    return array


def silu_slope(values):
    sigmoid_value = jax.nn.sigmoid(values)
    return sigmoid_value * (1.0 + values * (1.0 - sigmoid_value))


def product(form, left, right):
    return jnp.einsum(form, left, right, preferred_element_type=jnp.float32)


def dequantize(stored, scales):
    user_count, row_count, model_width = stored.shape
    block_count, head_count = (scales.shape[1], scales.shape[2])
    shaped = stored.astype(jnp.float32).reshape(
        user_count, block_count, row_count // block_count, head_count, model_width // head_count
    )
    scaled = shaped * scales[:, :, None, :, None]
    return scaled.astype(jnp.bfloat16).reshape(user_count * row_count, model_width)


def key_mask(user_ids, lengths, shard_index, hist_rows, span_rows):
    query_count = user_ids.shape[0]
    user_count = lengths.shape[0]
    key_index = jnp.arange(user_count * hist_rows, dtype=jnp.int32)
    key_user = key_index // hist_rows
    key_row = shard_index * hist_rows + key_index % hist_rows
    user_range = jnp.arange(user_count, dtype=jnp.int32)
    key_limit = jnp.sum(
        jnp.where(key_user[:, None] == user_range[None, :], lengths[None, :], 0), axis=1
    )
    history_mask = (user_ids[:, None] == key_user[None, :]) & (key_row < key_limit)[None, :]
    span_start = shard_index * span_rows
    span_pos = span_start + jnp.arange(span_rows, dtype=jnp.int32)
    span_users = lax.dynamic_slice_in_dim(user_ids, span_start, span_rows, 0)
    query_pos = jnp.arange(query_count, dtype=jnp.int32)
    span_mask = (user_ids[:, None] == span_users[None, :]) & (
        span_pos[None, :] <= query_pos[:, None]
    )
    return jnp.concatenate([history_mask, span_mask], axis=1)


def split_heads(matrix, head_count):
    return matrix.reshape(matrix.shape[0], head_count, matrix.shape[1] // head_count)


def forward_part(queries, keys, values_all, mask, head_count):
    head_size = queries.shape[1] // head_count
    scores = product(
        "qhd,khd->hqk", split_heads(queries, head_count), split_heads(keys, head_count)
    ) / math.sqrt(head_size)
    attn = jnp.where(mask[None], jax.nn.silu(scores), 0.0).astype(jnp.bfloat16)
    mixed = product("hqk,khd->qhd", attn, split_heads(values_all, head_count))
    weighted_slope = jnp.where(mask[None], silu_slope(scores), 0.0) / math.sqrt(head_size)
    return (mixed.reshape(queries.shape[0], queries.shape[1]), weighted_slope)


def backward_part(keys, values_all, weighted_slope, mixed_grad, head_count):
    attn_grad = product(
        "qhd,khd->hqk", split_heads(mixed_grad, head_count), split_heads(values_all, head_count)
    )
    score_grad = (attn_grad * weighted_slope).astype(jnp.bfloat16)
    query_grad = product("hqk,khd->qhd", score_grad, split_heads(keys, head_count))
    return query_grad.reshape(mixed_grad.shape[0], mixed_grad.shape[1])


def shards(
    tokens,
    gate_values,
    output_grad,
    query_weight,
    master,
    moment,
    second,
    key_codes,
    value_codes,
    key_scales,
    value_scales,
    span_keys,
    span_values,
    lengths,
    segments,
):
    model_width = query_weight.shape[0]
    shard_index = lax.axis_index(CACHE)
    features = collect_cache(tokens, 1)
    query_pre = jnp.dot(features, query_weight, preferred_element_type=jnp.float32) / math.sqrt(
        model_width
    )
    query_block = jax.nn.silu(query_pre).astype(jnp.bfloat16)
    queries = collect_cache(query_block, 1)
    user_ids = segments[0]
    hist_rows = key_codes.shape[1]
    span_rows = span_keys.shape[0]
    keys = jnp.concatenate([dequantize(key_codes, key_scales), span_keys], axis=0)
    values_all = jnp.concatenate([dequantize(value_codes, value_scales), span_values], axis=0)
    mask = key_mask(user_ids, lengths, shard_index, hist_rows, span_rows)
    mixed_part, weighted_slope = forward_part(queries, keys, values_all, mask, HEADS)
    gate_float = gate_values.astype(jnp.float32)
    mixed_block = summed_over_cache(mixed_part, 1)
    back = output_grad.astype(jnp.float32) * gate_float
    row_sum, row_square, back_sum, back_mixed = packed_total(
        (
            jnp.sum(mixed_block, axis=1),
            jnp.sum(mixed_block * mixed_block, axis=1),
            jnp.sum(back, axis=1),
            jnp.sum(back * mixed_block, axis=1),
        ),
        CACHE,
    )
    row_mean = (row_sum / model_width)[:, None]
    row_var = (row_square / model_width)[:, None] - row_mean * row_mean
    inverse = 1.0 / jnp.sqrt(row_var + 1e-05)
    normed = (mixed_block - row_mean) * inverse
    layer_block = (gate_float * normed).astype(jnp.bfloat16)
    back_cross = inverse[:, 0] * (back_mixed - row_mean[:, 0] * back_sum)
    grad_block = inverse * (
        back - (back_sum / model_width)[:, None] - normed * (back_cross / model_width)[:, None]
    )
    mixed_grad = collect_cache(grad_block.astype(jnp.bfloat16), 1)
    query_part = backward_part(keys, values_all, weighted_slope, mixed_grad, HEADS)
    query_grad = rounded_sum_over_cache(query_part, 1)
    pre_grad = (query_grad * silu_slope(query_pre)).astype(jnp.bfloat16)
    weight_part = lax.dot_general(
        features, pre_grad, (((0,), (0,)), ((), ())), preferred_element_type=jnp.float32
    ) / math.sqrt(model_width)
    grad_owned = sent_and_summed(weight_part.astype(jnp.bfloat16), DP, 0)
    square_total = of_everyone(jnp.sum(grad_owned * grad_owned).reshape(1), CACHE_DP)[0]
    grad_level = jnp.sqrt(square_total / (model_width * model_width))
    clip_factor = jnp.minimum(1.0, 0.5 / (grad_level + 1e-06))
    clipped = clip_factor * grad_owned
    new_moment = 0.9 * moment + 0.1 * clipped
    new_second = 0.95 * second + 0.05 * clipped * clipped
    first_fix = new_moment / (1.0 - 0.9**STEP)
    second_fix = new_second / (1.0 - 0.95**STEP)
    new_master = master - 0.01 * (first_fix / (jnp.sqrt(second_fix) + 1e-08) + 0.1 * master)
    new_weight = collect(new_master.astype(jnp.bfloat16), DP, 0)
    return (layer_block, new_weight, new_master, new_moment, new_second)


def solution(mesh):
    torus = Mesh(
        mesh.devices.reshape(2, 8, 2, 8, 2), ("cache_0", "cache_1", "cache_2", "dp_0", "dp_1")
    )
    placed = (
        P(DP, CACHE),
        P(DP, CACHE),
        P(DP, CACHE),
        P(None, CACHE),
        P(DP, CACHE),
        P(DP, CACHE),
        P(DP, CACHE),
        P(DP, CACHE, None),
        P(DP, CACHE, None),
        P(DP, CACHE, None),
        P(DP, CACHE, None),
        P(DP_CACHE, None),
        P(DP_CACHE, None),
        P(DP),
        P(DP, None),
    )
    return jax.shard_map(
        shards,
        mesh=torus,
        in_specs=placed,
        out_specs=(P(DP, CACHE), P(None, CACHE), P(DP, CACHE), P(DP, CACHE), P(DP, CACHE)),
        check_vma=False,
    )
```

```python
import math

import jax
import jax.numpy as jnp
from jax import lax
from jax.sharding import Mesh
from jax.sharding import PartitionSpec as P

HEADS = 16
STEP = 20
CACHE = ("cache_0", "cache_1", "cache_2")
DP = ("dp_0", "dp_1")
CACHE_DP = ("cache_0", "cache_1", "cache_2", "dp_0", "dp_1")
DP_CACHE = ("dp_0", "dp_1", "cache_0", "cache_1", "cache_2")


def split_up(array, dim, peers):
    dims = array.shape
    tiles = array.reshape(*dims[:dim], peers, dims[dim] // peers, *dims[dim + 1 :])
    return jnp.moveaxis(tiles, dim, 0)


def summed_on_arrival(array, axis, dim):
    tiles = split_up(array, dim, lax.axis_size(axis))
    arrived = lax.all_to_all(tiles, axis, split_axis=0, concat_axis=0, tiled=True)
    return arrived.sum(axis=0)


def sent_to_all(array, axis):
    copies = jnp.broadcast_to(array, (lax.axis_size(axis), *array.shape))
    return lax.all_to_all(copies, axis, split_axis=0, concat_axis=0, tiled=True)


def of_everyone(array, axis):
    everything = sent_to_all(array, axis)
    return jnp.sum(everything, axis=0)


def packed_total(arrays, axis):
    flat, at, outs = (jnp.concatenate([a.reshape(-1) for a in arrays]), 0, [])
    subtotal = of_everyone(flat, axis)
    for a in arrays:
        outs.append(subtotal[at : at + a.size].reshape(a.shape))
        at += a.size
    return tuple(outs)


def in_order(tiles, dim):
    dims = list(tiles.shape[1:])
    dims[dim] *= tiles.shape[0]
    return jnp.moveaxis(tiles, 0, dim).reshape(dims)


CHIPS = ("cache_0", "cache_1")
CORE = "cache_2"


def partner(array):
    return lax.ppermute(array, CORE, [(0, 1), (1, 0)])


def by_core(tiles):
    first = lax.axis_index(CORE) == 0
    return (jnp.where(first, tiles[0], tiles[1]), jnp.where(first, tiles[1], tiles[0]))


def collect_cache_early(array, dim):
    chips = lax.axis_size(CHIPS)
    across = lax.all_to_all(
        jnp.broadcast_to(array, (chips, *array.shape)), CHIPS, 0, 0, tiled=True
    )
    cores = lax.axis_size(CORE)
    pairs = lax.all_to_all(
        jnp.broadcast_to(across, (cores, *across.shape)), CORE, 0, 0, tiled=True
    )
    tiles = jnp.swapaxes(pairs, 0, 1).reshape(chips * cores, *array.shape)
    return in_order(tiles, dim)


def collect_cache(array, dim):
    chips = lax.axis_size(CHIPS)
    across = lax.all_to_all(
        jnp.broadcast_to(array, (chips, *array.shape)), CHIPS, 0, 0, tiled=True
    )
    other = partner(across)
    first = lax.axis_index(CORE) == 0
    pairs = jnp.stack([jnp.where(first, across, other), jnp.where(first, other, across)])
    tiles = jnp.swapaxes(pairs, 0, 1).reshape(2 * chips, *array.shape)
    return in_order(tiles, dim)


def summed_over_cache(array, dim):
    chips, cores = (lax.axis_size(CHIPS), lax.axis_size(CORE))
    tiles = split_up(array, dim, chips * cores)
    tiles = jnp.swapaxes(tiles.reshape(chips, cores, *tiles.shape[1:]), 0, 1)
    kept, sent = by_core(tiles)
    on_chip = kept + partner(sent)
    return lax.all_to_all(on_chip, CHIPS, 0, 0, tiled=True).sum(axis=0)


def rounded_sum_over_cache(array, dim):
    chips, cores = (lax.axis_size(CHIPS), lax.axis_size(CORE))
    tiles = split_up(array.astype(jnp.bfloat16), dim, chips * cores)
    tiles = jnp.swapaxes(tiles.reshape(chips, cores, *tiles.shape[1:]), 0, 1)
    kept, sent = by_core(tiles)
    pair_sum = kept.astype(jnp.float32) + partner(sent).astype(jnp.float32)
    arrived = lax.all_to_all(pair_sum.astype(jnp.bfloat16), CHIPS, 0, 0, tiled=True)
    return jnp.sum(arrived.astype(jnp.float32), axis=0)


def collect(array, axis, dim):
    tiles = sent_to_all(array, axis)
    return in_order(tiles, dim)


def sent_and_summed(array, axis, dim):
    peers = lax.axis_size(axis)
    tiles = lax.all_to_all(split_up(array, dim, peers), axis, 0, 0, tiled=True)
    return jnp.sum(tiles.astype(jnp.float32), axis=0)


def by_axis(array, axes):
    for axis in axes:
        array = lax.psum(array, axis)
    return array


def silu_slope(values):
    sigmoid_value = jax.nn.sigmoid(values)
    return sigmoid_value * (1.0 + values * (1.0 - sigmoid_value))


def product(form, left, right):
    return jnp.einsum(form, left, right, preferred_element_type=jnp.float32)


def dequantize(stored, scales):
    user_count, row_count, model_width = stored.shape
    block_count, head_count = (scales.shape[1], scales.shape[2])
    shaped = stored.astype(jnp.float32).reshape(
        user_count, block_count, row_count // block_count, head_count, model_width // head_count
    )
    scaled = shaped * scales[:, :, None, :, None]
    return scaled.astype(jnp.bfloat16).reshape(user_count * row_count, model_width)


def key_mask(user_ids, lengths, shard_index, hist_rows, span_rows):
    query_count = user_ids.shape[0]
    user_count = lengths.shape[0]
    key_index = jnp.arange(user_count * hist_rows, dtype=jnp.int32)
    key_user = key_index // hist_rows
    key_row = shard_index * hist_rows + key_index % hist_rows
    user_range = jnp.arange(user_count, dtype=jnp.int32)
    key_limit = jnp.sum(
        jnp.where(key_user[:, None] == user_range[None, :], lengths[None, :], 0), axis=1
    )
    history_mask = (user_ids[:, None] == key_user[None, :]) & (key_row < key_limit)[None, :]
    span_start = shard_index * span_rows
    span_pos = span_start + jnp.arange(span_rows, dtype=jnp.int32)
    span_users = lax.dynamic_slice_in_dim(user_ids, span_start, span_rows, 0)
    query_pos = jnp.arange(query_count, dtype=jnp.int32)
    span_mask = (user_ids[:, None] == span_users[None, :]) & (
        span_pos[None, :] <= query_pos[:, None]
    )
    return jnp.concatenate([history_mask, span_mask], axis=1)


def split_heads(matrix, head_count):
    return matrix.reshape(matrix.shape[0], head_count, matrix.shape[1] // head_count)


def forward_part(queries, keys, values_all, mask, head_count):
    head_size = queries.shape[1] // head_count
    scores = product(
        "qhd,khd->hqk", split_heads(queries, head_count), split_heads(keys, head_count)
    ) / math.sqrt(head_size)
    attn = jnp.where(mask[None], jax.nn.silu(scores), 0.0).astype(jnp.bfloat16)
    mixed = product("hqk,khd->qhd", attn, split_heads(values_all, head_count))
    weighted_slope = jnp.where(mask[None], silu_slope(scores), 0.0) / math.sqrt(head_size)
    return (mixed.reshape(queries.shape[0], queries.shape[1]), weighted_slope)


def backward_part(keys, values_all, weighted_slope, mixed_grad, head_count):
    attn_grad = product(
        "qhd,khd->hqk", split_heads(mixed_grad, head_count), split_heads(values_all, head_count)
    )
    score_grad = (attn_grad * weighted_slope).astype(jnp.bfloat16)
    query_grad = product("hqk,khd->qhd", score_grad, split_heads(keys, head_count))
    return query_grad.reshape(mixed_grad.shape[0], mixed_grad.shape[1])


def shards(
    tokens,
    gate_values,
    output_grad,
    query_weight,
    master,
    moment,
    second,
    key_codes,
    value_codes,
    key_scales,
    value_scales,
    span_keys,
    span_values,
    lengths,
    segments,
):
    model_width = query_weight.shape[0]
    shard_index = lax.axis_index(CACHE)
    features = collect_cache_early(tokens, 1)
    query_pre = jnp.dot(features, query_weight, preferred_element_type=jnp.float32) / math.sqrt(
        model_width
    )
    query_block = jax.nn.silu(query_pre).astype(jnp.bfloat16)
    queries = collect_cache_early(query_block, 1)
    user_ids = segments[0]
    hist_rows = key_codes.shape[1]
    span_rows = span_keys.shape[0]
    keys = jnp.concatenate([dequantize(key_codes, key_scales), span_keys], axis=0)
    values_all = jnp.concatenate([dequantize(value_codes, value_scales), span_values], axis=0)
    mask = key_mask(user_ids, lengths, shard_index, hist_rows, span_rows)
    mixed_part, weighted_slope = forward_part(queries, keys, values_all, mask, HEADS)
    gate_float = gate_values.astype(jnp.float32)
    mixed_block = summed_over_cache(mixed_part, 1)
    back = output_grad.astype(jnp.float32) * gate_float
    row_sum, row_square, back_sum, back_mixed = packed_total(
        (
            jnp.sum(mixed_block, axis=1),
            jnp.sum(mixed_block * mixed_block, axis=1),
            jnp.sum(back, axis=1),
            jnp.sum(back * mixed_block, axis=1),
        ),
        CACHE,
    )
    row_mean = (row_sum / model_width)[:, None]
    row_var = (row_square / model_width)[:, None] - row_mean * row_mean
    inverse = 1.0 / jnp.sqrt(row_var + 1e-05)
    normed = (mixed_block - row_mean) * inverse
    layer_block = (gate_float * normed).astype(jnp.bfloat16)
    back_cross = inverse[:, 0] * (back_mixed - row_mean[:, 0] * back_sum)
    grad_block = inverse * (
        back - (back_sum / model_width)[:, None] - normed * (back_cross / model_width)[:, None]
    )
    mixed_grad = collect_cache(grad_block.astype(jnp.bfloat16), 1)
    query_part = backward_part(keys, values_all, weighted_slope, mixed_grad, HEADS)
    query_grad = rounded_sum_over_cache(query_part, 1)
    pre_grad = (query_grad * silu_slope(query_pre)).astype(jnp.bfloat16)
    weight_part = lax.dot_general(
        features, pre_grad, (((0,), (0,)), ((), ())), preferred_element_type=jnp.float32
    ) / math.sqrt(model_width)
    grad_owned = sent_and_summed(weight_part.astype(jnp.bfloat16), DP, 0)
    square_total = of_everyone(jnp.sum(grad_owned * grad_owned).reshape(1), CACHE_DP)[0]
    grad_level = jnp.sqrt(square_total / (model_width * model_width))
    clip_factor = jnp.minimum(1.0, 0.5 / (grad_level + 1e-06))
    clipped = clip_factor * grad_owned
    new_moment = 0.9 * moment + 0.1 * clipped
    new_second = 0.95 * second + 0.05 * clipped * clipped
    first_fix = new_moment / (1.0 - 0.9**STEP)
    second_fix = new_second / (1.0 - 0.95**STEP)
    new_master = master - 0.01 * (first_fix / (jnp.sqrt(second_fix) + 1e-08) + 0.1 * master)
    new_weight = collect(new_master.astype(jnp.bfloat16), DP, 0)
    return (layer_block, new_weight, new_master, new_moment, new_second)


def solution(mesh):
    torus = Mesh(
        mesh.devices.reshape(2, 8, 2, 8, 2), ("cache_0", "cache_1", "cache_2", "dp_0", "dp_1")
    )
    placed = (
        P(DP, CACHE),
        P(DP, CACHE),
        P(DP, CACHE),
        P(None, CACHE),
        P(DP, CACHE),
        P(DP, CACHE),
        P(DP, CACHE),
        P(DP, CACHE, None),
        P(DP, CACHE, None),
        P(DP, CACHE, None),
        P(DP, CACHE, None),
        P(DP_CACHE, None),
        P(DP_CACHE, None),
        P(DP),
        P(DP, None),
    )
    return jax.shard_map(
        shards,
        mesh=torus,
        in_specs=placed,
        out_specs=(P(DP, CACHE), P(None, CACHE), P(DP, CACHE), P(DP, CACHE), P(DP, CACHE)),
        check_vma=False,
    )
```

```python
import math

import jax
import jax.numpy as jnp
from jax import lax
from jax.sharding import Mesh
from jax.sharding import PartitionSpec as P

HEADS = 16
STEP = 20
CACHE = ("cache_0", "cache_1", "cache_2")
DP = ("dp_0", "dp_1")
CACHE_DP = ("cache_0", "cache_1", "cache_2", "dp_0", "dp_1")
DP_CACHE = ("dp_0", "dp_1", "cache_0", "cache_1", "cache_2")


def split_up(array, dim, peers):
    dims = array.shape
    tiles = array.reshape(*dims[:dim], peers, dims[dim] // peers, *dims[dim + 1 :])
    return jnp.moveaxis(tiles, dim, 0)


def summed_on_arrival(array, axis, dim):
    tiles = split_up(array, dim, lax.axis_size(axis))
    arrived = lax.all_to_all(tiles, axis, split_axis=0, concat_axis=0, tiled=True)
    return arrived.sum(axis=0)


def sent_to_all(array, axis):
    copies = jnp.broadcast_to(array, (lax.axis_size(axis), *array.shape))
    return lax.all_to_all(copies, axis, split_axis=0, concat_axis=0, tiled=True)


def of_everyone(array, axis):
    everything = sent_to_all(array, axis)
    return jnp.sum(everything, axis=0)


def packed_total(arrays, axis):
    flat, at, outs = (jnp.concatenate([a.reshape(-1) for a in arrays]), 0, [])
    subtotal = of_everyone(flat, axis)
    for a in arrays:
        outs.append(subtotal[at : at + a.size].reshape(a.shape))
        at += a.size
    return tuple(outs)


def in_order(tiles, dim):
    dims = list(tiles.shape[1:])
    dims[dim] *= tiles.shape[0]
    return jnp.moveaxis(tiles, 0, dim).reshape(dims)


CHIPS = ("cache_0", "cache_1")
CORE = "cache_2"


def partner(array):
    return lax.ppermute(array, CORE, [(0, 1), (1, 0)])


def by_core(tiles):
    first = lax.axis_index(CORE) == 0
    return (jnp.where(first, tiles[0], tiles[1]), jnp.where(first, tiles[1], tiles[0]))


def collect_cache_early(array, dim):
    chips = lax.axis_size(CHIPS)
    across = lax.all_to_all(
        jnp.broadcast_to(array, (chips, *array.shape)), CHIPS, 0, 0, tiled=True
    )
    cores = lax.axis_size(CORE)
    pairs = lax.all_to_all(
        jnp.broadcast_to(across, (cores, *across.shape)), CORE, 0, 0, tiled=True
    )
    tiles = jnp.swapaxes(pairs, 0, 1).reshape(chips * cores, *array.shape)
    return in_order(tiles, dim)


def collect_cache(array, dim):
    chips = lax.axis_size(CHIPS)
    across = lax.all_to_all(
        jnp.broadcast_to(array, (chips, *array.shape)), CHIPS, 0, 0, tiled=True
    )
    other = partner(across)
    first = lax.axis_index(CORE) == 0
    pairs = jnp.stack([jnp.where(first, across, other), jnp.where(first, other, across)])
    tiles = jnp.swapaxes(pairs, 0, 1).reshape(2 * chips, *array.shape)
    return in_order(tiles, dim)


def summed_over_cache(array, dim):
    chips, cores = (lax.axis_size(CHIPS), lax.axis_size(CORE))
    tiles = split_up(array, dim, chips * cores)
    tiles = jnp.swapaxes(tiles.reshape(chips, cores, *tiles.shape[1:]), 0, 1)
    kept, sent = by_core(tiles)
    on_chip = kept + partner(sent)
    return lax.all_to_all(on_chip, CHIPS, 0, 0, tiled=True).sum(axis=0)


def rounded_sum_over_cache(array, dim):
    chips, cores = (lax.axis_size(CHIPS), lax.axis_size(CORE))
    tiles = split_up(array.astype(jnp.bfloat16), dim, chips * cores)
    tiles = jnp.swapaxes(tiles.reshape(chips, cores, *tiles.shape[1:]), 0, 1)
    kept, sent = by_core(tiles)
    pair_sum = kept.astype(jnp.float32) + partner(sent).astype(jnp.float32)
    arrived = lax.all_to_all(pair_sum.astype(jnp.bfloat16), CHIPS, 0, 0, tiled=True)
    return jnp.sum(arrived.astype(jnp.float32), axis=0)


def collect(array, axis, dim):
    tiles = sent_to_all(array, axis)
    return in_order(tiles, dim)


def sent_and_summed(array, axis, dim):
    peers = lax.axis_size(axis)
    tiles = lax.all_to_all(split_up(array, dim, peers), axis, 0, 0, tiled=True)
    return jnp.sum(tiles.astype(jnp.float32), axis=0)


def by_axis(array, axes):
    for axis in axes:
        array = lax.psum(array, axis)
    return array


def silu_slope(values):
    sigmoid_value = jax.nn.sigmoid(values)
    return sigmoid_value * (1.0 + values * (1.0 - sigmoid_value))


def product(form, left, right):
    return jnp.einsum(form, left, right, preferred_element_type=jnp.float32)


def dequantize(stored, scales):
    user_count, row_count, model_width = stored.shape
    block_count, head_count = (scales.shape[1], scales.shape[2])
    shaped = stored.astype(jnp.float32).reshape(
        user_count, block_count, row_count // block_count, head_count, model_width // head_count
    )
    scaled = shaped * scales[:, :, None, :, None]
    return scaled.astype(jnp.bfloat16).reshape(user_count * row_count, model_width)


def key_mask(user_ids, lengths, shard_index, hist_rows, span_rows):
    query_count = user_ids.shape[0]
    user_count = lengths.shape[0]
    key_index = jnp.arange(user_count * hist_rows, dtype=jnp.int32)
    key_user = key_index // hist_rows
    key_row = shard_index * hist_rows + key_index % hist_rows
    user_range = jnp.arange(user_count, dtype=jnp.int32)
    key_limit = jnp.sum(
        jnp.where(key_user[:, None] == user_range[None, :], lengths[None, :], 0), axis=1
    )
    history_mask = (user_ids[:, None] == key_user[None, :]) & (key_row < key_limit)[None, :]
    span_start = shard_index * span_rows
    span_pos = span_start + jnp.arange(span_rows, dtype=jnp.int32)
    span_users = lax.dynamic_slice_in_dim(user_ids, span_start, span_rows, 0)
    query_pos = jnp.arange(query_count, dtype=jnp.int32)
    span_mask = (user_ids[:, None] == span_users[None, :]) & (
        span_pos[None, :] <= query_pos[:, None]
    )
    return jnp.concatenate([history_mask, span_mask], axis=1)


def split_heads(matrix, head_count):
    return matrix.reshape(matrix.shape[0], head_count, matrix.shape[1] // head_count)


def forward_part(queries, keys, values_all, mask, head_count):
    head_size = queries.shape[1] // head_count
    scores = product(
        "qhd,khd->hqk", split_heads(queries, head_count), split_heads(keys, head_count)
    ) / math.sqrt(head_size)
    attn = jnp.where(mask[None], jax.nn.silu(scores), 0.0).astype(jnp.bfloat16)
    mixed = product("hqk,khd->qhd", attn, split_heads(values_all, head_count))
    weighted_slope = jnp.where(mask[None], silu_slope(scores), 0.0) / math.sqrt(head_size)
    return (mixed.reshape(queries.shape[0], queries.shape[1]), weighted_slope)


def backward_part(keys, values_all, weighted_slope, mixed_grad, head_count):
    attn_grad = product(
        "qhd,khd->hqk", split_heads(mixed_grad, head_count), split_heads(values_all, head_count)
    )
    score_grad = (attn_grad * weighted_slope).astype(jnp.bfloat16)
    query_grad = product("hqk,khd->qhd", score_grad, split_heads(keys, head_count))
    return query_grad.reshape(mixed_grad.shape[0], mixed_grad.shape[1])


def shards(
    tokens,
    gate_values,
    output_grad,
    query_weight,
    master,
    moment,
    second,
    key_codes,
    value_codes,
    key_scales,
    value_scales,
    span_keys,
    span_values,
    lengths,
    segments,
):
    model_width = query_weight.shape[0]
    shard_index = lax.axis_index(CACHE)
    features = collect_cache_early(tokens, 1)
    query_pre = jnp.dot(features, query_weight, preferred_element_type=jnp.float32) / math.sqrt(
        model_width
    )
    query_block = jax.nn.silu(query_pre).astype(jnp.bfloat16)
    queries = collect_cache(query_block, 1)
    user_ids = segments[0]
    hist_rows = key_codes.shape[1]
    span_rows = span_keys.shape[0]
    keys = jnp.concatenate([dequantize(key_codes, key_scales), span_keys], axis=0)
    values_all = jnp.concatenate([dequantize(value_codes, value_scales), span_values], axis=0)
    mask = key_mask(user_ids, lengths, shard_index, hist_rows, span_rows)
    mixed_part, weighted_slope = forward_part(queries, keys, values_all, mask, HEADS)
    gate_float = gate_values.astype(jnp.float32)
    mixed_block = summed_over_cache(mixed_part, 1)
    back = output_grad.astype(jnp.float32) * gate_float
    row_sum, row_square, back_sum, back_mixed = packed_total(
        (
            jnp.sum(mixed_block, axis=1),
            jnp.sum(mixed_block * mixed_block, axis=1),
            jnp.sum(back, axis=1),
            jnp.sum(back * mixed_block, axis=1),
        ),
        CACHE,
    )
    row_mean = (row_sum / model_width)[:, None]
    row_var = (row_square / model_width)[:, None] - row_mean * row_mean
    inverse = 1.0 / jnp.sqrt(row_var + 1e-05)
    normed = (mixed_block - row_mean) * inverse
    layer_block = (gate_float * normed).astype(jnp.bfloat16)
    back_cross = inverse[:, 0] * (back_mixed - row_mean[:, 0] * back_sum)
    grad_block = inverse * (
        back - (back_sum / model_width)[:, None] - normed * (back_cross / model_width)[:, None]
    )
    mixed_grad = collect_cache(grad_block.astype(jnp.bfloat16), 1)
    query_part = backward_part(keys, values_all, weighted_slope, mixed_grad, HEADS)
    query_grad = rounded_sum_over_cache(query_part, 1)
    pre_grad = (query_grad * silu_slope(query_pre)).astype(jnp.bfloat16)
    weight_part = lax.dot_general(
        features, pre_grad, (((0,), (0,)), ((), ())), preferred_element_type=jnp.float32
    ) / math.sqrt(model_width)
    grad_owned = sent_and_summed(weight_part.astype(jnp.bfloat16), DP, 0)
    square_total = of_everyone(jnp.sum(grad_owned * grad_owned).reshape(1), CACHE_DP)[0]
    grad_level = jnp.sqrt(square_total / (model_width * model_width))
    clip_factor = jnp.minimum(1.0, 0.5 / (grad_level + 1e-06))
    clipped = clip_factor * grad_owned
    new_moment = 0.9 * moment + 0.1 * clipped
    new_second = 0.95 * second + 0.05 * clipped * clipped
    first_fix = new_moment / (1.0 - 0.9**STEP)
    second_fix = new_second / (1.0 - 0.95**STEP)
    new_master = master - 0.01 * (first_fix / (jnp.sqrt(second_fix) + 1e-08) + 0.1 * master)
    new_weight = collect(new_master.astype(jnp.bfloat16), DP, 0)
    return (layer_block, new_weight, new_master, new_moment, new_second)


def solution(mesh):
    torus = Mesh(
        mesh.devices.reshape(2, 8, 2, 8, 2), ("cache_0", "cache_1", "cache_2", "dp_0", "dp_1")
    )
    placed = (
        P(DP, CACHE),
        P(DP, CACHE),
        P(DP, CACHE),
        P(None, CACHE),
        P(DP, CACHE),
        P(DP, CACHE),
        P(DP, CACHE),
        P(DP, CACHE, None),
        P(DP, CACHE, None),
        P(DP, CACHE, None),
        P(DP, CACHE, None),
        P(DP_CACHE, None),
        P(DP_CACHE, None),
        P(DP),
        P(DP, None),
    )
    return jax.shard_map(
        shards,
        mesh=torus,
        in_specs=placed,
        out_specs=(P(DP, CACHE), P(None, CACHE), P(DP, CACHE), P(DP, CACHE), P(DP, CACHE)),
        check_vma=False,
    )
```

```python
import math

import jax
import jax.numpy as jnp
from jax import lax
from jax.sharding import Mesh
from jax.sharding import PartitionSpec as P

HEADS = 16
STEP = 20
CACHE = ("cache_0", "cache_1", "cache_2")
DP = ("dp_0", "dp_1")
CACHE_DP = ("cache_0", "cache_1", "cache_2", "dp_0", "dp_1")
DP_CACHE = ("dp_0", "dp_1", "cache_0", "cache_1", "cache_2")


def split_up(array, dim, peers):
    dims = array.shape
    tiles = array.reshape(*dims[:dim], peers, dims[dim] // peers, *dims[dim + 1 :])
    return jnp.moveaxis(tiles, dim, 0)


def summed_on_arrival(array, axis, dim):
    tiles = split_up(array, dim, lax.axis_size(axis))
    arrived = lax.all_to_all(tiles, axis, split_axis=0, concat_axis=0, tiled=True)
    return arrived.sum(axis=0)


def sent_to_all(array, axis):
    copies = jnp.broadcast_to(array, (lax.axis_size(axis), *array.shape))
    return lax.all_to_all(copies, axis, split_axis=0, concat_axis=0, tiled=True)


def of_everyone(array, axis):
    everything = sent_to_all(array, axis)
    return jnp.sum(everything, axis=0)


def packed_total(arrays, axis):
    flat, at, outs = (jnp.concatenate([a.reshape(-1) for a in arrays]), 0, [])
    subtotal = of_everyone(flat, axis)
    for a in arrays:
        outs.append(subtotal[at : at + a.size].reshape(a.shape))
        at += a.size
    return tuple(outs)


def in_order(tiles, dim):
    dims = list(tiles.shape[1:])
    dims[dim] *= tiles.shape[0]
    return jnp.moveaxis(tiles, 0, dim).reshape(dims)


CHIPS = ("cache_0", "cache_1")
CORE = "cache_2"


def partner(array):
    return lax.ppermute(array, CORE, [(0, 1), (1, 0)])


def by_core(tiles):
    first = lax.axis_index(CORE) == 0
    return (jnp.where(first, tiles[0], tiles[1]), jnp.where(first, tiles[1], tiles[0]))


def collect_cache_early(array, dim):
    chips = lax.axis_size(CHIPS)
    across = lax.all_to_all(
        jnp.broadcast_to(array, (chips, *array.shape)), CHIPS, 0, 0, tiled=True
    )
    cores = lax.axis_size(CORE)
    pairs = lax.all_to_all(
        jnp.broadcast_to(across, (cores, *across.shape)), CORE, 0, 0, tiled=True
    )
    tiles = jnp.swapaxes(pairs, 0, 1).reshape(chips * cores, *array.shape)
    return in_order(tiles, dim)


def collect_cache(array, dim):
    chips = lax.axis_size(CHIPS)
    across = lax.all_to_all(
        jnp.broadcast_to(array, (chips, *array.shape)), CHIPS, 0, 0, tiled=True
    )
    other = partner(across)
    first = lax.axis_index(CORE) == 0
    pairs = jnp.stack([jnp.where(first, across, other), jnp.where(first, other, across)])
    tiles = jnp.swapaxes(pairs, 0, 1).reshape(2 * chips, *array.shape)
    return in_order(tiles, dim)


def summed_over_cache(array, dim):
    chips, cores = (lax.axis_size(CHIPS), lax.axis_size(CORE))
    tiles = split_up(array, dim, chips * cores)
    tiles = jnp.swapaxes(tiles.reshape(chips, cores, *tiles.shape[1:]), 0, 1)
    kept, sent = by_core(tiles)
    on_chip = kept + partner(sent)
    return lax.all_to_all(on_chip, CHIPS, 0, 0, tiled=True).sum(axis=0)


def rounded_sum_over_cache(array, dim):
    chips, cores = (lax.axis_size(CHIPS), lax.axis_size(CORE))
    tiles = split_up(array.astype(jnp.bfloat16), dim, chips * cores)
    tiles = jnp.swapaxes(tiles.reshape(chips, cores, *tiles.shape[1:]), 0, 1)
    kept, sent = by_core(tiles)
    pair_sum = kept.astype(jnp.float32) + partner(sent).astype(jnp.float32)
    arrived = lax.all_to_all(pair_sum.astype(jnp.bfloat16), CHIPS, 0, 0, tiled=True)
    return jnp.sum(arrived.astype(jnp.float32), axis=0)


def collect(array, axis, dim):
    tiles = sent_to_all(array, axis)
    return in_order(tiles, dim)


def sent_and_summed(array, axis, dim):
    peers = lax.axis_size(axis)
    tiles = lax.all_to_all(split_up(array, dim, peers), axis, 0, 0, tiled=True)
    return jnp.sum(tiles.astype(jnp.float32), axis=0)


def by_axis(array, axes):
    for axis in axes:
        array = lax.psum(array, axis)
    return array


def silu_slope(values):
    sigmoid_value = jax.nn.sigmoid(values)
    return sigmoid_value * (1.0 + values * (1.0 - sigmoid_value))


def product(form, left, right):
    return jnp.einsum(form, left, right, preferred_element_type=jnp.float32)


def dequantize(stored, scales):
    user_count, row_count, model_width = stored.shape
    block_count, head_count = (scales.shape[1], scales.shape[2])
    shaped = stored.astype(jnp.float32).reshape(
        user_count, block_count, row_count // block_count, head_count, model_width // head_count
    )
    scaled = shaped * scales[:, :, None, :, None]
    return scaled.astype(jnp.bfloat16).reshape(user_count * row_count, model_width)


def key_mask(user_ids, lengths, shard_index, hist_rows, span_rows):
    query_count = user_ids.shape[0]
    user_count = lengths.shape[0]
    key_index = jnp.arange(user_count * hist_rows, dtype=jnp.int32)
    key_user = key_index // hist_rows
    key_row = shard_index * hist_rows + key_index % hist_rows
    user_range = jnp.arange(user_count, dtype=jnp.int32)
    key_limit = jnp.sum(
        jnp.where(key_user[:, None] == user_range[None, :], lengths[None, :], 0), axis=1
    )
    history_mask = (user_ids[:, None] == key_user[None, :]) & (key_row < key_limit)[None, :]
    span_start = shard_index * span_rows
    span_pos = span_start + jnp.arange(span_rows, dtype=jnp.int32)
    span_users = lax.dynamic_slice_in_dim(user_ids, span_start, span_rows, 0)
    query_pos = jnp.arange(query_count, dtype=jnp.int32)
    span_mask = (user_ids[:, None] == span_users[None, :]) & (
        span_pos[None, :] <= query_pos[:, None]
    )
    return jnp.concatenate([history_mask, span_mask], axis=1)


def split_heads(matrix, head_count):
    return matrix.reshape(matrix.shape[0], head_count, matrix.shape[1] // head_count)


def forward_part(queries, keys, values_all, mask, head_count):
    head_size = queries.shape[1] // head_count
    scores = product(
        "qhd,khd->hqk", split_heads(queries, head_count), split_heads(keys, head_count)
    ) / math.sqrt(head_size)
    attn = jnp.where(mask[None], jax.nn.silu(scores), 0.0).astype(jnp.bfloat16)
    mixed = product("hqk,khd->qhd", attn, split_heads(values_all, head_count))
    weighted_slope = jnp.where(mask[None], silu_slope(scores), 0.0) / math.sqrt(head_size)
    return (mixed.reshape(queries.shape[0], queries.shape[1]), weighted_slope)


def backward_part(keys, values_all, weighted_slope, mixed_grad, head_count):
    attn_grad = product(
        "qhd,khd->hqk", split_heads(mixed_grad, head_count), split_heads(values_all, head_count)
    )
    score_grad = (attn_grad * weighted_slope).astype(jnp.bfloat16)
    query_grad = product("hqk,khd->qhd", score_grad, split_heads(keys, head_count))
    return query_grad.reshape(mixed_grad.shape[0], mixed_grad.shape[1])


def shards(
    tokens,
    gate_values,
    output_grad,
    query_weight,
    master,
    moment,
    second,
    key_codes,
    value_codes,
    key_scales,
    value_scales,
    span_keys,
    span_values,
    lengths,
    segments,
):
    model_width = query_weight.shape[0]
    shard_index = lax.axis_index(CACHE)
    features = collect_cache_early(tokens, 1)
    query_pre = jnp.dot(features, query_weight, preferred_element_type=jnp.float32) / math.sqrt(
        model_width
    )
    query_block = jax.nn.silu(query_pre).astype(jnp.bfloat16)
    queries = collect_cache_early(query_block, 1)
    user_ids = segments[0]
    hist_rows = key_codes.shape[1]
    span_rows = span_keys.shape[0]
    keys = jnp.concatenate([dequantize(key_codes, key_scales), span_keys], axis=0)
    values_all = jnp.concatenate([dequantize(value_codes, value_scales), span_values], axis=0)
    mask = key_mask(user_ids, lengths, shard_index, hist_rows, span_rows)
    mixed_part, weighted_slope = forward_part(queries, keys, values_all, mask, HEADS)
    gate_float = gate_values.astype(jnp.float32)
    mixed_block = summed_over_cache(mixed_part, 1)
    back = output_grad.astype(jnp.float32) * gate_float
    row_sum, row_square, back_sum, back_mixed = packed_total(
        (
            jnp.sum(mixed_block, axis=1),
            jnp.sum(mixed_block * mixed_block, axis=1),
            jnp.sum(back, axis=1),
            jnp.sum(back * mixed_block, axis=1),
        ),
        CACHE,
    )
    row_mean = (row_sum / model_width)[:, None]
    row_var = (row_square / model_width)[:, None] - row_mean * row_mean
    inverse = 1.0 / jnp.sqrt(row_var + 1e-05)
    normed = (mixed_block - row_mean) * inverse
    layer_block = (gate_float * normed).astype(jnp.bfloat16)
    back_cross = inverse[:, 0] * (back_mixed - row_mean[:, 0] * back_sum)
    grad_block = inverse * (
        back - (back_sum / model_width)[:, None] - normed * (back_cross / model_width)[:, None]
    )
    mixed_grad = collect_cache(grad_block.astype(jnp.bfloat16), 1)
    query_part = backward_part(keys, values_all, weighted_slope, mixed_grad, HEADS)
    query_grad = rounded_sum_over_cache(query_part, 1)
    pre_grad = (query_grad * silu_slope(query_pre)).astype(jnp.bfloat16)
    weight_part = lax.dot_general(
        features, pre_grad, (((0,), (0,)), ((), ())), preferred_element_type=jnp.float32
    ) / math.sqrt(model_width)
    grad_owned = sent_and_summed(weight_part.astype(jnp.bfloat16), DP, 0)
    square_pair = jnp.sum(grad_owned * grad_owned).reshape(1)
    square_pair = square_pair + partner(square_pair)
    square_total = of_everyone(square_pair, CHIPS + DP)[0]
    grad_level = jnp.sqrt(square_total / (model_width * model_width))
    clip_factor = jnp.minimum(1.0, 0.5 / (grad_level + 1e-06))
    clipped = clip_factor * grad_owned
    new_moment = 0.9 * moment + 0.1 * clipped
    new_second = 0.95 * second + 0.05 * clipped * clipped
    first_fix = new_moment / (1.0 - 0.9**STEP)
    second_fix = new_second / (1.0 - 0.95**STEP)
    new_master = master - 0.01 * (first_fix / (jnp.sqrt(second_fix) + 1e-08) + 0.1 * master)
    new_weight = collect(new_master.astype(jnp.bfloat16), DP, 0)
    return (layer_block, new_weight, new_master, new_moment, new_second)


def solution(mesh):
    torus = Mesh(
        mesh.devices.reshape(2, 8, 2, 8, 2), ("cache_0", "cache_1", "cache_2", "dp_0", "dp_1")
    )
    placed = (
        P(DP, CACHE),
        P(DP, CACHE),
        P(DP, CACHE),
        P(None, CACHE),
        P(DP, CACHE),
        P(DP, CACHE),
        P(DP, CACHE),
        P(DP, CACHE, None),
        P(DP, CACHE, None),
        P(DP, CACHE, None),
        P(DP, CACHE, None),
        P(DP_CACHE, None),
        P(DP_CACHE, None),
        P(DP),
        P(DP, None),
    )
    return jax.shard_map(
        shards,
        mesh=torus,
        in_specs=placed,
        out_specs=(P(DP, CACHE), P(None, CACHE), P(DP, CACHE), P(DP, CACHE), P(DP, CACHE)),
        check_vma=False,
    )
```
